512 devices in a mesh: win: 16 (over z_hi, y, core), tm: 32 (over z_lo, x).
Axes of the slice: x: 4, y: 4, z: 16 (z_hi: 2, z_lo: 8; z = z_hi * 8 + z_lo), core: 2. Of those that a mesh axis runs over, the one named last changes fastest.
Arguments:
- frame_inputs: bfloat16 [16, 4096, 2048], P('win', 'tm'), may hold values from -6 to 6
- gate_channels: bfloat16 [16, 4096, 2048], P('win', 'tm'), may hold values from -6 to 6
- state_input_weight: bfloat16 [16, 4096, 128], P('win', 'tm'), may hold values from -6 to 6
- state_output_weight: bfloat16 [16, 4096, 128], P('win', 'tm'), may hold values from -0.59765625 to 0.59765625
- head_decay_codes: int32 [2, 32], replicated, may hold values from 0 to 7
- loss_frames: int32 [16, 4096], P('win', 'tm'), may hold values 0 or 1
- gated_norm_gain: float32 [2048], replicated, may hold values from 0.1 to 1.9
- output_weight: bfloat16 [2048, 1024], P(None, 'tm'), may hold values from -0.125 to 0.125
- seam_taper_shape: int32 [16], replicated, may hold values from 0 to 3
Outputs:
- mixed: bfloat16 [16, 4096, 1024], P('win', 'tm')
The draws below stay inside these ranges and needn't reach their ends.
All inputs are finite; a program needn't handle non-finite values. No bound on the sum of `loss_frames` on one device may be relied on, other than what follows from the above.
Results may differ from the reference program's by a relative error of at most 0.0059.
Values may be sent and summed in bfloat16 or wider, within the bound.
No kernel may reach another device: no remote copies, remote signals or barrier semaphores. Data moves between devices by JAX's collectives and lax.ppermute only.
A program may use at most 192 MiB of HBM per device.

```python
import jax
import jax.numpy as jnp
from jax import lax

D = 1024
H = 32
P_SIZE = 64
N = 128
FR_DEV = 128
HP = 2048
WINDOW_COUNT = 16
WINDOW_FRAMES = 4096
SEAM = 512
STRIDE = 3584
N_TM = 32


def plant(drawn, key, smallest, high):
    longest = drawn.shape.index(max(drawn.shape))
    spots = []
    for shift in (0, 1):
        where = [jax.random.randint(jax.random.fold_in(key, axis), (), 0, length) for axis, length in enumerate(drawn.shape)]
        where[longest] = (where[longest] + shift) % drawn.shape[longest]
        spots.append(tuple(where))
    return drawn.at[spots[0]].set(smallest).at[spots[1]].set(high)


def levels(own_key, extent, cuts, least, top_value):
    gain, own = 1.0, jax.random.fold_in(own_key, 6)
    for dim, blocks in cuts:
        draws = jnp.exp(jax.random.uniform(jax.random.fold_in(own, dim), (blocks,), jnp.float32, least / len(cuts), top_value / len(cuts)))
        gain = gain * jnp.repeat(draws, extent[dim] // blocks).reshape([-1 if axis == dim else 1 for axis in range(len(extent))])
    return gain


def normal_values(stream_key, extent, deviation, most, cuts=(), kind=jnp.bfloat16):
    drawn = deviation * jax.random.normal(stream_key, extent, jnp.float32)
    if cuts:
        drawn = drawn * levels(stream_key, extent, cuts, -0.22, 0.18)
    return jnp.clip(drawn, -most, most).astype(kind)


def setup_inputs(seed: int = 0) -> dict:
    seeds = jax.random.split(jax.random.key(seed), 10)
    return {
        "frame_inputs": normal_values(seeds[0], (WINDOW_COUNT, WINDOW_FRAMES, HP), 1.0, 6.0, ((0, 16), (1, 32))),
        "gate_channels": normal_values(seeds[1], (WINDOW_COUNT, WINDOW_FRAMES, HP), 1.0, 6.0, ((0, 16), (1, 32))),
        "state_input_weight": normal_values(seeds[2], (WINDOW_COUNT, WINDOW_FRAMES, N), 1.0, 6.0, ((0, 16), (1, 32))),
        "state_output_weight": normal_values(seeds[3], (WINDOW_COUNT, WINDOW_FRAMES, N), 0.09, 0.59765625, ((0, 16), (1, 32))),
        "head_decay_codes": plant(jax.random.randint(seeds[4], (2, H), 0, 8), jax.random.fold_in(seeds[4], 1), 0, 7).astype(jnp.int32),
        "loss_frames": plant((jax.random.randint(seeds[5], (WINDOW_COUNT, WINDOW_FRAMES), 0, 4096) < 1).astype(jnp.int32), jax.random.fold_in(seeds[5], 1), 0, 1),
        "gated_norm_gain": jnp.clip(1.0 + 0.18 * jax.random.normal(seeds[6], (HP,), jnp.float32), 0.1, 1.9),
        "output_weight": normal_values(seeds[7], (HP, D), HP ** -0.5, 0.125, ((1, 32),)),
        "seam_taper_shape": plant(jax.random.randint(seeds[8], (WINDOW_COUNT,), 0, 4), jax.random.fold_in(seeds[8], 1), 0, 3).astype(jnp.int32),
    }


STATE_LOSS = 0.4
EPSILON = 1e-05

def decay_rates(head_decay_codes, window_length):
    codes_float = head_decay_codes.astype(jnp.float32)
    quick = jnp.exp2(-codes_float) / 32.0
    gentle = jnp.exp2(5.0 - codes_float) / window_length
    return jnp.where(head_decay_codes < 4, quick, gentle)

def taper_weight(taper_code, position, seam_length):
    spread = (position.astype(jnp.float32) + 0.5) / seam_length
    shapes = jnp.stack([spread, spread * spread * (3.0 - 2.0 * spread), jnp.sin(0.5 * jnp.pi * spread) ** 2, spread ** 3 * (spread * (6.0 * spread - 15.0) + 10.0)])
    kind_index = jnp.arange(4).reshape((4,) + (1,) * spread.ndim)
    selected = kind_index == jnp.expand_dims(taper_code, 0)
    return lax.optimization_barrier(jnp.sum(jnp.where(selected, shapes, 0.0), axis=0))

def forward_block(state_in, frames, b_rows, c_rows, log_decay):
    running = jnp.cumsum(log_decay, axis=0)
    scores = jnp.dot(c_rows, b_rows.T, preferred_element_type=jnp.float32)
    count = running.shape[0]
    lower_mask = jnp.arange(count)[:, None] >= jnp.arange(count)[None, :]
    spread = running.T[:, :, None] - running.T[:, None, :]
    weights = jnp.exp(jnp.where(lower_mask[None], spread, -jnp.inf))
    mixing = (scores[None] * weights).astype(jnp.bfloat16)
    local_part = jnp.einsum('hts,shp->thp', mixing.astype(jnp.float32), frames.astype(jnp.float32))
    carried = jnp.exp(running)[:, :, None] * jnp.einsum('hpn,tn->thp', state_in, c_rows.astype(jnp.float32), precision=lax.Precision.HIGHEST)
    to_end = jnp.exp(running[-1][None, :] - running)
    weighted_b = (to_end[:, :, None] * b_rows.astype(jnp.float32)[:, None, :]).astype(jnp.bfloat16)
    fresh_state = jnp.einsum('shp,shn->hpn', frames.astype(jnp.float32), weighted_b.astype(jnp.float32))
    new_state = jnp.exp(running[-1])[:, None, None] * state_in + fresh_state
    return (new_state, local_part + carried)

def backward_block(state_in, frames, b_rows, c_rows, log_decay):
    running = jnp.flip(jnp.cumsum(jnp.flip(log_decay, 0), axis=0), 0)
    scores = jnp.dot(c_rows, b_rows.T, preferred_element_type=jnp.float32)
    count = running.shape[0]
    upper_mask = jnp.arange(count)[:, None] < jnp.arange(count)[None, :]
    spread = running.T[:, :, None] - running.T[:, None, :]
    weights = jnp.exp(jnp.where(upper_mask[None], spread, -jnp.inf))
    mixing = (scores[None] * weights).astype(jnp.bfloat16)
    local_part = jnp.einsum('hts,shp->thp', mixing.astype(jnp.float32), frames.astype(jnp.float32))
    carried = jnp.exp(running)[:, :, None] * jnp.einsum('hpn,tn->thp', state_in, c_rows.astype(jnp.float32), precision=lax.Precision.HIGHEST)
    to_start = jnp.exp(running[0][None, :] - running)
    weighted_b = (to_start[:, :, None] * b_rows.astype(jnp.float32)[:, None, :]).astype(jnp.bfloat16)
    fresh_state = jnp.einsum('shp,shn->hpn', frames.astype(jnp.float32), weighted_b.astype(jnp.float32))
    new_state = jnp.exp(running[0])[:, None, None] * state_in + fresh_state
    return (new_state, local_part + carried)

def reference(frame_inputs, gate_channels, state_input_weight, state_output_weight, head_decay_codes, loss_frames, gated_norm_gain, output_weight, seam_taper_shape):
    decay_rate_pair = decay_rates(head_decay_codes, WINDOW_FRAMES)

    def window_result(window_items):
        frames, gates, b_all, c_all, marks = window_items
        loss_float = marks.astype(jnp.float32)[:, None]
        forward_log_decay = -(decay_rate_pair[0][None, :] + STATE_LOSS * loss_float)
        backward_log_decay = -(decay_rate_pair[1][None, :] + STATE_LOSS * loss_float)
        block_frames = frames.reshape(N_TM, FR_DEV, H, P_SIZE)
        block_b = b_all.reshape(N_TM, FR_DEV, N)
        block_c = c_all.reshape(N_TM, FR_DEV, N)
        start_state = jnp.zeros((H, P_SIZE, N), jnp.float32)

        def forward_step(state_in, block_items):
            return forward_block(state_in, *block_items)

        def backward_step(state_in, block_items):
            return backward_block(state_in, *block_items)
        forward_items = (block_frames, block_b, block_c, forward_log_decay.reshape(N_TM, FR_DEV, H))
        backward_items = (block_frames, block_b, block_c, backward_log_decay.reshape(N_TM, FR_DEV, H))
        _, forward_out = lax.scan(forward_step, start_state, forward_items)
        _, backward_out = lax.scan(backward_step, start_state, backward_items, reverse=True)
        summed = (forward_out + backward_out).reshape(WINDOW_FRAMES, H, P_SIZE)
        gated_rows = summed * jax.nn.silu(gates.astype(jnp.float32)).reshape(WINDOW_FRAMES, H, P_SIZE)
        inverse_rms = lax.rsqrt(lax.optimization_barrier(jnp.mean(gated_rows * gated_rows, axis=-1, keepdims=True)) + EPSILON)
        normed = ((gated_rows * inverse_rms).reshape(WINDOW_FRAMES, H * P_SIZE) * gated_norm_gain[None, :]).astype(jnp.bfloat16)
        return jnp.dot(normed, output_weight, preferred_element_type=jnp.float32).astype(jnp.bfloat16)
    projected_rows = lax.map(window_result, (frame_inputs, gate_channels, state_input_weight, state_output_weight, loss_frames))
    own_rows = projected_rows.astype(jnp.float32)
    positions = jnp.arange(SEAM)
    fade_in = taper_weight(seam_taper_shape[1:, None], positions[None, :], SEAM)[:, :, None]
    blended = fade_in * own_rows[1:, :SEAM] + (1.0 - fade_in) * own_rows[:-1, STRIDE:]
    mixed = own_rows.at[1:, :SEAM].set(blended).at[:-1, STRIDE:].set(blended)
    return mixed.astype(jnp.bfloat16)
```

```python
import jax
import jax.numpy as jnp
from jax import lax
from jax.sharding import Mesh
from jax.sharding import PartitionSpec as P

H = 32
P_SIZE = 64
N = 128
SEAM_DEVS = 4
ROW = 4
PAD_ROWS = 8

STATE_LOSS = 0.4
EPSILON = 1e-05


def decay_rates(head_decay_codes, window_length):
    codes_float = head_decay_codes.astype(jnp.float32)
    quick = jnp.exp2(-codes_float) / 32.0
    gentle = jnp.exp2(5.0 - codes_float) / window_length
    return jnp.where(head_decay_codes < 4, quick, gentle)


def taper_weight(taper_code, position, seam_length):
    spread = (position.astype(jnp.float32) + 0.5) / seam_length
    shapes = jnp.stack(
        [
            spread,
            spread * spread * (3.0 - 2.0 * spread),
            jnp.sin(0.5 * jnp.pi * spread) ** 2,
            spread**3 * (spread * (6.0 * spread - 15.0) + 10.0),
        ]
    )
    kind_index = jnp.arange(4).reshape((4,) + (1,) * spread.ndim)
    selected = kind_index == jnp.expand_dims(taper_code, 0)
    return jnp.sum(jnp.where(selected, shapes, 0.0), axis=0)


def combine(earlier, later):
    return (earlier[0] + later[0], jnp.exp(later[0])[..., None, None] * earlier[1] + later[1])


def shift(value, axis, by):
    count = lax.axis_size(axis)
    pairs = [(i, i + by) for i in range(count) if 0 <= i + by < count]
    return lax.ppermute(value, axis, pairs)


def split_packed(packed):
    return packed[..., P_SIZE, 0], packed[..., :P_SIZE, :]


def pack(logs, states):
    rows = jnp.broadcast_to(logs[..., None, None], logs.shape + (PAD_ROWS, N))
    return jnp.concatenate([states, rows], axis=-2)


def scan_states(log_fwd, log_bwd, fresh_fwd, fresh_bwd):
    packed = pack(jnp.stack([log_fwd, log_bwd]), jnp.stack([fresh_fwd, fresh_bwd]))
    groups = lax.axis_size("x")
    per_group = H // groups
    packed = packed.reshape(2, groups, per_group, P_SIZE + PAD_ROWS, N)
    mine = lax.all_to_all(packed, "x", 1, 1, tiled=True)
    logs, states = split_packed(mine)
    zero_l = jnp.zeros_like(logs[:, 0])
    zero_s = jnp.zeros_like(states[:, 0])
    fwd_pre = []
    acc = (zero_l[0], zero_s[0])
    for k in range(ROW):
        fwd_pre.append(acc)
        acc = combine(acc, (logs[0, k], states[0, k]))
    fwd_total = acc
    bwd_pre = [None] * ROW
    acc = (zero_l[1], zero_s[1])
    for k in reversed(range(ROW)):
        bwd_pre[k] = acc
        acc = combine(acc, (logs[1, k], states[1, k]))
    bwd_total = acc
    rows = lax.axis_size("z")

    def column_scan(total, step):
        carried = shift(pack(*total), "z", step)
        d = 1
        while d < rows - 1:
            got = shift(carried, "z", step * d)
            carried = pack(*combine(split_packed(got), split_packed(carried)))
            d *= 2
        return split_packed(carried)

    fwd_in = column_scan(fwd_total, 1)
    bwd_in = column_scan(bwd_total, -1)
    out_f = jnp.stack([combine(fwd_in, fwd_pre[k])[1] for k in range(ROW)])
    out_b = jnp.stack([combine(bwd_in, bwd_pre[k])[1] for k in range(ROW)])
    out = jnp.stack([out_f, out_b])
    back = lax.all_to_all(out, "x", 1, 1, tiled=True)
    back = back.reshape(2, H, P_SIZE, N)
    return back[0], back[1]


def per_device(
    frame_inputs,
    gate_channels,
    state_input_weight,
    state_output_weight,
    head_decay_codes,
    loss_frames,
    gated_norm_gain,
    output_weight,
    seam_taper_shape,
):
    frames = frame_inputs[0]
    frame_count = frames.shape[0]
    rows = lax.axis_size("z")
    row_len = lax.axis_size("x")
    chain_length = rows * row_len
    window_length = frame_count * chain_length
    seam_length = SEAM_DEVS * frame_count
    group_count = H // 4
    decay_rate_pair = decay_rates(head_decay_codes, window_length)
    loss_float = loss_frames[0].astype(jnp.float32)[:, None]
    forward_log_decay = -(decay_rate_pair[0][None, :] + STATE_LOSS * loss_float)
    backward_log_decay = -(decay_rate_pair[1][None, :] + STATE_LOSS * loss_float)
    running_fwd = jnp.cumsum(forward_log_decay, axis=0)
    running_bwd = jnp.flip(jnp.cumsum(jnp.flip(backward_log_decay, 0), axis=0), 0)
    b_rows = state_input_weight[0]
    c_rows = state_output_weight[0]
    head_frames = frames.reshape(frame_count, H, P_SIZE)
    b_float = b_rows.astype(jnp.float32)[:, None, :]
    weighted_fwd = (jnp.exp(running_fwd[-1][None, :] - running_fwd)[:, :, None] * b_float).astype(
        jnp.bfloat16
    )
    weighted_bwd = (jnp.exp(running_bwd[0][None, :] - running_bwd)[:, :, None] * b_float).astype(
        jnp.bfloat16
    )
    fresh_fwd = jnp.einsum(
        "shp,shn->hpn", head_frames, weighted_fwd, preferred_element_type=jnp.float32
    )
    fresh_bwd = jnp.einsum(
        "shp,shn->hpn", head_frames, weighted_bwd, preferred_element_type=jnp.float32
    )
    state_fwd, state_bwd = scan_states(running_fwd[-1], running_bwd[0], fresh_fwd, fresh_bwd)
    scores = jnp.dot(c_rows, b_rows.T, preferred_element_type=jnp.float32)
    lower_mask = jnp.arange(frame_count)[:, None] >= jnp.arange(frame_count)[None, :]

    def group_mix(group_items):
        group_fwd, group_bwd, group_frames = group_items
        exponent = jnp.where(
            lower_mask[None],
            group_fwd[:, :, None] - group_fwd[:, None, :],
            group_bwd[:, :, None] - group_bwd[:, None, :],
        )
        mixing = (scores[None] * jnp.exp(exponent)).astype(jnp.bfloat16)
        return jnp.einsum("hts,shp->thp", mixing, group_frames, preferred_element_type=jnp.float32)

    grouped_fwd = running_fwd.T.reshape(group_count, 4, frame_count)
    grouped_bwd = running_bwd.T.reshape(group_count, 4, frame_count)
    grouped_frames = head_frames.reshape(frame_count, group_count, 4, P_SIZE).transpose(1, 0, 2, 3)
    local_groups = lax.map(group_mix, (grouped_fwd, grouped_bwd, grouped_frames))
    local_part = local_groups.transpose(1, 0, 2, 3).reshape(frame_count, H, P_SIZE)
    c_float = c_rows.astype(jnp.float32)
    carried_fwd = jnp.exp(running_fwd)[:, :, None] * jnp.einsum(
        "hpn,tn->thp", state_fwd, c_float, precision=lax.Precision.HIGHEST
    )
    carried_bwd = jnp.exp(running_bwd)[:, :, None] * jnp.einsum(
        "hpn,tn->thp", state_bwd, c_float, precision=lax.Precision.HIGHEST
    )
    summed = local_part + carried_fwd + carried_bwd
    gated_rows = summed * jax.nn.silu(gate_channels[0].astype(jnp.float32)).reshape(
        frame_count, H, P_SIZE
    )
    inverse_rms = lax.rsqrt(jnp.mean(gated_rows * gated_rows, axis=-1, keepdims=True) + EPSILON)
    normed = (
        (gated_rows * inverse_rms).reshape(frame_count, H * P_SIZE) * gated_norm_gain[None, :]
    ).astype(jnp.bfloat16)
    projected_rows = jnp.dot(
        normed,
        lax.all_gather(output_weight, ("z", "x"), axis=1, tiled=True),
        preferred_element_type=jnp.float32,
    ).astype(jnp.bfloat16)
    window_index = lax.axis_index("win")
    window_total = lax.axis_size("win")
    row_index = lax.axis_index("z")
    pairs = []
    for w in range(1, window_total):
        pairs.append(((w - 1) * rows + rows - 1, w * rows))
        pairs.append((w * rows, (w - 1) * rows + rows - 1))
    partner = lax.ppermute(projected_rows, ("win", "z"), pairs)
    seam_pos = lax.axis_index("x") * frame_count + jnp.arange(frame_count)
    is_tail = row_index == rows - 1
    fade_window = jnp.minimum(window_index + is_tail.astype(jnp.int32), window_total - 1)
    fade = taper_weight(seam_taper_shape[fade_window], seam_pos, seam_length)[:, None]
    own_rows = projected_rows.astype(jnp.float32)
    other_rows = partner.astype(jnp.float32)
    head_mix = fade * own_rows + (1.0 - fade) * other_rows
    tail_mix = fade * other_rows + (1.0 - fade) * own_rows
    use_head = (row_index == 0) & (window_index > 0)
    use_tail = is_tail & (window_index < window_total - 1)
    mixed = jnp.where(use_head, head_mix, jnp.where(use_tail, tail_mix, own_rows))
    return mixed.astype(jnp.bfloat16)[None]


def solution(mesh):
    wins, chain = mesh.devices.shape
    rows = chain // ROW
    grid = Mesh(mesh.devices.reshape(wins, rows, ROW), ("win", "z", "x"))
    blocks = ("z", "x")
    in_specs = (
        P("win", blocks, None),
        P("win", blocks, None),
        P("win", blocks, None),
        P("win", blocks, None),
        P(),
        P("win", blocks),
        P(),
        P(None, blocks),
        P(),
    )
    out_specs = P("win", blocks, None)
    return jax.shard_map(
        per_device, mesh=grid, in_specs=in_specs, out_specs=out_specs, check_vma=False
    )
```

```python
import jax
import jax.numpy as jnp
from jax import lax
from jax.sharding import Mesh
from jax.sharding import PartitionSpec as P

H = 32
P_SIZE = 64
N = 128
SEAM_DEVS = 4
ROW = 4
PAD_ROWS = 8

STATE_LOSS = 0.4
EPSILON = 1e-05


def decay_rates(head_decay_codes, window_length):
    codes_float = head_decay_codes.astype(jnp.float32)
    quick = jnp.exp2(-codes_float) / 32.0
    gentle = jnp.exp2(5.0 - codes_float) / window_length
    return jnp.where(head_decay_codes < 4, quick, gentle)


def taper_weight(taper_code, position, seam_length):
    spread = (position.astype(jnp.float32) + 0.5) / seam_length
    shapes = jnp.stack(
        [
            spread,
            spread * spread * (3.0 - 2.0 * spread),
            jnp.sin(0.5 * jnp.pi * spread) ** 2,
            spread**3 * (spread * (6.0 * spread - 15.0) + 10.0),
        ]
    )
    kind_index = jnp.arange(4).reshape((4,) + (1,) * spread.ndim)
    selected = kind_index == jnp.expand_dims(taper_code, 0)
    return jnp.sum(jnp.where(selected, shapes, 0.0), axis=0)


def combine(earlier, later):
    return (earlier[0] + later[0], jnp.exp(later[0])[..., None, None] * earlier[1] + later[1])


def shift(value, axis, by):
    count = lax.axis_size(axis)
    pairs = [(i, i + by) for i in range(count) if 0 <= i + by < count]
    return lax.ppermute(value, axis, pairs)


def split_packed(packed):
    return packed[..., P_SIZE, 0], packed[..., :P_SIZE, :]


def pack(logs, states):
    rows = jnp.broadcast_to(logs[..., None, None], logs.shape + (PAD_ROWS, N))
    return jnp.concatenate([states, rows], axis=-2)


def scan_states(log_fwd, log_bwd, fresh_fwd, fresh_bwd):
    packed = pack(jnp.stack([log_fwd, log_bwd]), jnp.stack([fresh_fwd, fresh_bwd]))
    groups = lax.axis_size("x")
    per_group = H // groups
    packed = packed.reshape(2, groups, per_group, P_SIZE + PAD_ROWS, N)
    mine = lax.all_to_all(packed, "x", 1, 1, tiled=True)
    logs, states = split_packed(mine)
    zero_l = jnp.zeros_like(logs[:, 0])
    zero_s = jnp.zeros_like(states[:, 0])
    fwd_pre = []
    acc = (zero_l[0], zero_s[0])
    for k in range(ROW):
        fwd_pre.append(acc)
        acc = combine(acc, (logs[0, k], states[0, k]))
    fwd_total = acc
    bwd_pre = [None] * ROW
    acc = (zero_l[1], zero_s[1])
    for k in reversed(range(ROW)):
        bwd_pre[k] = acc
        acc = combine(acc, (logs[1, k], states[1, k]))
    bwd_total = acc
    rows = lax.axis_size("z")

    def column_scan(total, step):
        carried = shift(pack(*total), "z", step)
        d = 1
        while d < rows - 1:
            got = shift(carried, "z", step * d)
            carried = pack(*combine(split_packed(got), split_packed(carried)))
            d *= 2
        return split_packed(carried)

    fwd_in = column_scan(fwd_total, 1)
    bwd_in = column_scan(bwd_total, -1)
    out_f = jnp.stack([combine(fwd_in, fwd_pre[k])[1] for k in range(ROW)])
    out_b = jnp.stack([combine(bwd_in, bwd_pre[k])[1] for k in range(ROW)])
    out = jnp.stack([out_f, out_b])
    back = lax.all_to_all(out, "x", 1, 1, tiled=True)
    back = back.reshape(2, H, P_SIZE, N)
    return back[0], back[1]


def gather_weight(output_weight):
    column = lax.all_gather(output_weight, "z", axis=0)
    row = lax.all_gather(column, "x", axis=1)
    return row.transpose(2, 0, 1, 3).reshape(output_weight.shape[0], -1)


def per_device(
    frame_inputs,
    gate_channels,
    state_input_weight,
    state_output_weight,
    head_decay_codes,
    loss_frames,
    gated_norm_gain,
    output_weight,
    seam_taper_shape,
):
    frames = frame_inputs[0]
    frame_count = frames.shape[0]
    rows = lax.axis_size("z")
    row_len = lax.axis_size("x")
    chain_length = rows * row_len
    window_length = frame_count * chain_length
    seam_length = SEAM_DEVS * frame_count
    group_count = H // 4
    decay_rate_pair = decay_rates(head_decay_codes, window_length)
    loss_float = loss_frames[0].astype(jnp.float32)[:, None]
    forward_log_decay = -(decay_rate_pair[0][None, :] + STATE_LOSS * loss_float)
    backward_log_decay = -(decay_rate_pair[1][None, :] + STATE_LOSS * loss_float)
    running_fwd = jnp.cumsum(forward_log_decay, axis=0)
    running_bwd = jnp.flip(jnp.cumsum(jnp.flip(backward_log_decay, 0), axis=0), 0)
    b_rows = state_input_weight[0]
    c_rows = state_output_weight[0]
    head_frames = frames.reshape(frame_count, H, P_SIZE)
    b_float = b_rows.astype(jnp.float32)[:, None, :]
    weighted_fwd = (jnp.exp(running_fwd[-1][None, :] - running_fwd)[:, :, None] * b_float).astype(
        jnp.bfloat16
    )
    weighted_bwd = (jnp.exp(running_bwd[0][None, :] - running_bwd)[:, :, None] * b_float).astype(
        jnp.bfloat16
    )
    fresh_fwd = jnp.einsum(
        "shp,shn->hpn", head_frames, weighted_fwd, preferred_element_type=jnp.float32
    )
    fresh_bwd = jnp.einsum(
        "shp,shn->hpn", head_frames, weighted_bwd, preferred_element_type=jnp.float32
    )
    state_fwd, state_bwd = scan_states(running_fwd[-1], running_bwd[0], fresh_fwd, fresh_bwd)
    scores = jnp.dot(c_rows, b_rows.T, preferred_element_type=jnp.float32)
    lower_mask = jnp.arange(frame_count)[:, None] >= jnp.arange(frame_count)[None, :]

    def group_mix(group_items):
        group_fwd, group_bwd, group_frames = group_items
        exponent = jnp.where(
            lower_mask[None],
            group_fwd[:, :, None] - group_fwd[:, None, :],
            group_bwd[:, :, None] - group_bwd[:, None, :],
        )
        mixing = (scores[None] * jnp.exp(exponent)).astype(jnp.bfloat16)
        return jnp.einsum("hts,shp->thp", mixing, group_frames, preferred_element_type=jnp.float32)

    grouped_fwd = running_fwd.T.reshape(group_count, 4, frame_count)
    grouped_bwd = running_bwd.T.reshape(group_count, 4, frame_count)
    grouped_frames = head_frames.reshape(frame_count, group_count, 4, P_SIZE).transpose(1, 0, 2, 3)
    local_groups = lax.map(group_mix, (grouped_fwd, grouped_bwd, grouped_frames))
    local_part = local_groups.transpose(1, 0, 2, 3).reshape(frame_count, H, P_SIZE)
    c_float = c_rows.astype(jnp.float32)
    carried_fwd = jnp.exp(running_fwd)[:, :, None] * jnp.einsum(
        "hpn,tn->thp", state_fwd, c_float, precision=lax.Precision.HIGHEST
    )
    carried_bwd = jnp.exp(running_bwd)[:, :, None] * jnp.einsum(
        "hpn,tn->thp", state_bwd, c_float, precision=lax.Precision.HIGHEST
    )
    summed = local_part + carried_fwd + carried_bwd
    gated_rows = summed * jax.nn.silu(gate_channels[0].astype(jnp.float32)).reshape(
        frame_count, H, P_SIZE
    )
    inverse_rms = lax.rsqrt(jnp.mean(gated_rows * gated_rows, axis=-1, keepdims=True) + EPSILON)
    normed = (
        (gated_rows * inverse_rms).reshape(frame_count, H * P_SIZE) * gated_norm_gain[None, :]
    ).astype(jnp.bfloat16)
    projected_rows = jnp.dot(
        normed,
        gather_weight(output_weight),
        preferred_element_type=jnp.float32,
    ).astype(jnp.bfloat16)
    window_index = lax.axis_index("win")
    window_total = lax.axis_size("win")
    row_index = lax.axis_index("z")
    pairs = []
    for w in range(1, window_total):
        pairs.append(((w - 1) * rows + rows - 1, w * rows))
        pairs.append((w * rows, (w - 1) * rows + rows - 1))
    partner = lax.ppermute(projected_rows, ("win", "z"), pairs)
    seam_pos = lax.axis_index("x") * frame_count + jnp.arange(frame_count)
    is_tail = row_index == rows - 1
    fade_window = jnp.minimum(window_index + is_tail.astype(jnp.int32), window_total - 1)
    fade = taper_weight(seam_taper_shape[fade_window], seam_pos, seam_length)[:, None]
    own_rows = projected_rows.astype(jnp.float32)
    other_rows = partner.astype(jnp.float32)
    head_mix = fade * own_rows + (1.0 - fade) * other_rows
    tail_mix = fade * other_rows + (1.0 - fade) * own_rows
    use_head = (row_index == 0) & (window_index > 0)
    use_tail = is_tail & (window_index < window_total - 1)
    mixed = jnp.where(use_head, head_mix, jnp.where(use_tail, tail_mix, own_rows))
    return mixed.astype(jnp.bfloat16)[None]


def solution(mesh):
    wins, chain = mesh.devices.shape
    rows = chain // ROW
    grid = Mesh(mesh.devices.reshape(wins, rows, ROW), ("win", "z", "x"))
    blocks = ("z", "x")
    in_specs = (
        P("win", blocks, None),
        P("win", blocks, None),
        P("win", blocks, None),
        P("win", blocks, None),
        P(),
        P("win", blocks),
        P(),
        P(None, blocks),
        P(),
    )
    out_specs = P("win", blocks, None)
    return jax.shard_map(
        per_device, mesh=grid, in_specs=in_specs, out_specs=out_specs, check_vma=False
    )
```

```python
import jax
import jax.numpy as jnp
from jax import lax
from jax.sharding import Mesh
from jax.sharding import PartitionSpec as P

H = 32
P_SIZE = 64
N = 128
SEAM_DEVS = 4
ROW = 4
PAD_ROWS = 8

STATE_LOSS = 0.4
EPSILON = 1e-05


def decay_rates(head_decay_codes, window_length):
    codes_float = head_decay_codes.astype(jnp.float32)
    quick = jnp.exp2(-codes_float) / 32.0
    gentle = jnp.exp2(5.0 - codes_float) / window_length
    return jnp.where(head_decay_codes < 4, quick, gentle)


def taper_weight(taper_code, position, seam_length):
    spread = (position.astype(jnp.float32) + 0.5) / seam_length
    shapes = jnp.stack(
        [
            spread,
            spread * spread * (3.0 - 2.0 * spread),
            jnp.sin(0.5 * jnp.pi * spread) ** 2,
            spread**3 * (spread * (6.0 * spread - 15.0) + 10.0),
        ]
    )
    kind_index = jnp.arange(4).reshape((4,) + (1,) * spread.ndim)
    selected = kind_index == jnp.expand_dims(taper_code, 0)
    return jnp.sum(jnp.where(selected, shapes, 0.0), axis=0)


def combine(earlier, later):
    return (earlier[0] + later[0], jnp.exp(later[0])[..., None, None] * earlier[1] + later[1])


def shift(value, axis, by):
    count = lax.axis_size(axis)
    pairs = [(i, i + by) for i in range(count) if 0 <= i + by < count]
    return lax.ppermute(value, axis, pairs)


def split_packed(packed):
    return packed[..., P_SIZE, 0], packed[..., :P_SIZE, :]


def pack(logs, states):
    rows = jnp.broadcast_to(logs[..., None, None], logs.shape + (PAD_ROWS, N))
    return jnp.concatenate([states, rows], axis=-2)


def scan_states(log_fwd, log_bwd, fresh_fwd, fresh_bwd):
    packed = pack(jnp.stack([log_fwd, log_bwd]), jnp.stack([fresh_fwd, fresh_bwd]))
    parts = lax.axis_size("x")
    per_part = 2 * H // parts
    packed = packed.reshape(parts, per_part, P_SIZE + PAD_ROWS, N)
    mine = lax.all_to_all(packed, "x", 0, 0, tiled=True)
    is_bwd = lax.axis_index("x") >= parts // 2
    ordered = jnp.where(is_bwd, mine[::-1], mine)
    logs, states = split_packed(ordered)
    acc = (jnp.zeros_like(logs[0]), jnp.zeros_like(states[0]))
    pre = []
    for k in range(ROW):
        pre.append(acc)
        acc = combine(acc, (logs[k], states[k]))
    rows = lax.axis_size("z")
    total = acc
    entering = (jnp.zeros_like(acc[0]), jnp.zeros_like(acc[1]))
    d = 1
    while d < rows:
        pairs = []
        for z in range(rows):
            for x in range(parts):
                to = z + d if x < parts // 2 else z - d
                if 0 <= to < rows:
                    pairs.append((z * parts + x, to * parts + x))
        got = split_packed(lax.ppermute(pack(*total), ("z", "x"), pairs))
        entering = combine(got, entering)
        if d * 2 < rows:
            total = combine(got, total)
        d *= 2
    out = jnp.stack([combine(entering, pre[k])[1] for k in range(ROW)])
    out = jnp.where(is_bwd, out[::-1], out)
    back = lax.all_to_all(out, "x", 0, 0, tiled=True)
    back = back.reshape(2, H, P_SIZE, N)
    return back[0], back[1]


def gather_weight(output_weight):
    column = lax.all_gather(output_weight, "z", axis=0)
    row = lax.all_gather(column, "x", axis=1)
    return row.transpose(2, 0, 1, 3).reshape(output_weight.shape[0], -1)


def per_device(
    frame_inputs,
    gate_channels,
    state_input_weight,
    state_output_weight,
    head_decay_codes,
    loss_frames,
    gated_norm_gain,
    output_weight,
    seam_taper_shape,
):
    frames = frame_inputs[0]
    frame_count = frames.shape[0]
    rows = lax.axis_size("z")
    row_len = lax.axis_size("x")
    chain_length = rows * row_len
    window_length = frame_count * chain_length
    seam_length = SEAM_DEVS * frame_count
    group_count = H // 4
    decay_rate_pair = decay_rates(head_decay_codes, window_length)
    loss_float = loss_frames[0].astype(jnp.float32)[:, None]
    forward_log_decay = -(decay_rate_pair[0][None, :] + STATE_LOSS * loss_float)
    backward_log_decay = -(decay_rate_pair[1][None, :] + STATE_LOSS * loss_float)
    running_fwd = jnp.cumsum(forward_log_decay, axis=0)
    running_bwd = jnp.flip(jnp.cumsum(jnp.flip(backward_log_decay, 0), axis=0), 0)
    b_rows = state_input_weight[0]
    c_rows = state_output_weight[0]
    head_frames = frames.reshape(frame_count, H, P_SIZE)
    b_float = b_rows.astype(jnp.float32)[:, None, :]
    weighted_fwd = (jnp.exp(running_fwd[-1][None, :] - running_fwd)[:, :, None] * b_float).astype(
        jnp.bfloat16
    )
    weighted_bwd = (jnp.exp(running_bwd[0][None, :] - running_bwd)[:, :, None] * b_float).astype(
        jnp.bfloat16
    )
    fresh_fwd = jnp.einsum(
        "shp,shn->hpn", head_frames, weighted_fwd, preferred_element_type=jnp.float32
    )
    fresh_bwd = jnp.einsum(
        "shp,shn->hpn", head_frames, weighted_bwd, preferred_element_type=jnp.float32
    )
    state_fwd, state_bwd = scan_states(running_fwd[-1], running_bwd[0], fresh_fwd, fresh_bwd)
    scores = jnp.dot(c_rows, b_rows.T, preferred_element_type=jnp.float32)
    lower_mask = jnp.arange(frame_count)[:, None] >= jnp.arange(frame_count)[None, :]

    def group_mix(group_items):
        group_fwd, group_bwd, group_frames = group_items
        exponent = jnp.where(
            lower_mask[None],
            group_fwd[:, :, None] - group_fwd[:, None, :],
            group_bwd[:, :, None] - group_bwd[:, None, :],
        )
        mixing = (scores[None] * jnp.exp(exponent)).astype(jnp.bfloat16)
        return jnp.einsum("hts,shp->thp", mixing, group_frames, preferred_element_type=jnp.float32)

    grouped_fwd = running_fwd.T.reshape(group_count, 4, frame_count)
    grouped_bwd = running_bwd.T.reshape(group_count, 4, frame_count)
    grouped_frames = head_frames.reshape(frame_count, group_count, 4, P_SIZE).transpose(1, 0, 2, 3)
    local_groups = lax.map(group_mix, (grouped_fwd, grouped_bwd, grouped_frames))
    local_part = local_groups.transpose(1, 0, 2, 3).reshape(frame_count, H, P_SIZE)
    c_float = c_rows.astype(jnp.float32)
    carried_fwd = jnp.exp(running_fwd)[:, :, None] * jnp.einsum(
        "hpn,tn->thp", state_fwd, c_float, precision=lax.Precision.HIGHEST
    )
    carried_bwd = jnp.exp(running_bwd)[:, :, None] * jnp.einsum(
        "hpn,tn->thp", state_bwd, c_float, precision=lax.Precision.HIGHEST
    )
    summed = local_part + carried_fwd + carried_bwd
    gated_rows = summed * jax.nn.silu(gate_channels[0].astype(jnp.float32)).reshape(
        frame_count, H, P_SIZE
    )
    inverse_rms = lax.rsqrt(jnp.mean(gated_rows * gated_rows, axis=-1, keepdims=True) + EPSILON)
    normed = (
        (gated_rows * inverse_rms).reshape(frame_count, H * P_SIZE) * gated_norm_gain[None, :]
    ).astype(jnp.bfloat16)
    projected_rows = jnp.dot(
        normed,
        gather_weight(output_weight),
        preferred_element_type=jnp.float32,
    ).astype(jnp.bfloat16)
    window_index = lax.axis_index("win")
    window_total = lax.axis_size("win")
    row_index = lax.axis_index("z")
    pairs = []
    for w in range(1, window_total):
        pairs.append(((w - 1) * rows + rows - 1, w * rows))
        pairs.append((w * rows, (w - 1) * rows + rows - 1))
    partner = lax.ppermute(projected_rows, ("win", "z"), pairs)
    seam_pos = lax.axis_index("x") * frame_count + jnp.arange(frame_count)
    is_tail = row_index == rows - 1
    fade_window = jnp.minimum(window_index + is_tail.astype(jnp.int32), window_total - 1)
    fade = taper_weight(seam_taper_shape[fade_window], seam_pos, seam_length)[:, None]
    own_rows = projected_rows.astype(jnp.float32)
    other_rows = partner.astype(jnp.float32)
    head_mix = fade * own_rows + (1.0 - fade) * other_rows
    tail_mix = fade * other_rows + (1.0 - fade) * own_rows
    use_head = (row_index == 0) & (window_index > 0)
    use_tail = is_tail & (window_index < window_total - 1)
    mixed = jnp.where(use_head, head_mix, jnp.where(use_tail, tail_mix, own_rows))
    return mixed.astype(jnp.bfloat16)[None]


def solution(mesh):
    wins, chain = mesh.devices.shape
    rows = chain // ROW
    grid = Mesh(mesh.devices.reshape(wins, rows, ROW), ("win", "z", "x"))
    blocks = ("z", "x")
    in_specs = (
        P("win", blocks, None),
        P("win", blocks, None),
        P("win", blocks, None),
        P("win", blocks, None),
        P(),
        P("win", blocks),
        P(),
        P(None, blocks),
        P(),
    )
    out_specs = P("win", blocks, None)
    return jax.shard_map(
        per_device, mesh=grid, in_specs=in_specs, out_specs=out_specs, check_vma=False
    )
```

```python
import jax
import jax.numpy as jnp
from jax import lax
from jax.sharding import Mesh
from jax.sharding import PartitionSpec as P

H = 32
P_SIZE = 64
N = 128
SEAM_DEVS = 4
ROW = 4
PAD_ROWS = 8

STATE_LOSS = 0.4
EPSILON = 1e-05


def decay_rates(head_decay_codes, window_length):
    codes_float = head_decay_codes.astype(jnp.float32)
    quick = jnp.exp2(-codes_float) / 32.0
    gentle = jnp.exp2(5.0 - codes_float) / window_length
    return jnp.where(head_decay_codes < 4, quick, gentle)


def taper_weight(taper_code, position, seam_length):
    spread = (position.astype(jnp.float32) + 0.5) / seam_length
    shapes = jnp.stack(
        [
            spread,
            spread * spread * (3.0 - 2.0 * spread),
            jnp.sin(0.5 * jnp.pi * spread) ** 2,
            spread**3 * (spread * (6.0 * spread - 15.0) + 10.0),
        ]
    )
    kind_index = jnp.arange(4).reshape((4,) + (1,) * spread.ndim)
    selected = kind_index == jnp.expand_dims(taper_code, 0)
    return jnp.sum(jnp.where(selected, shapes, 0.0), axis=0)


def combine(earlier, later):
    return (earlier[0] + later[0], jnp.exp(later[0])[..., None, None] * earlier[1] + later[1])


def shift(value, axis, by):
    count = lax.axis_size(axis)
    pairs = [(i, i + by) for i in range(count) if 0 <= i + by < count]
    return lax.ppermute(value, axis, pairs)


def split_packed(packed):
    return packed[..., P_SIZE, 0], packed[..., :P_SIZE, :]


def pack(logs, states):
    rows = jnp.broadcast_to(logs[..., None, None], logs.shape + (PAD_ROWS, N))
    return jnp.concatenate([states, rows], axis=-2)


def scan_states(log_fwd, log_bwd, fresh_fwd, fresh_bwd, output_weight):
    packed = pack(jnp.stack([log_fwd, log_bwd]), jnp.stack([fresh_fwd, fresh_bwd]))
    parts = lax.axis_size("x")
    per_part = 2 * H // parts
    state_len = per_part * (P_SIZE + PAD_ROWS) * N
    weight_flat = output_weight.astype(jnp.float32).reshape(1, -1)
    send = jnp.concatenate(
        [packed.reshape(parts, state_len), jnp.broadcast_to(weight_flat, (parts, weight_flat.shape[1]))],
        axis=1,
    )
    got = lax.all_to_all(send, "x", 0, 0, tiled=True)
    mine = got[:, :state_len].reshape(parts, per_part, P_SIZE + PAD_ROWS, N)
    weight_row = got[:, state_len:].reshape((parts,) + output_weight.shape).astype(jnp.bfloat16)
    is_bwd = lax.axis_index("x") >= parts // 2
    ordered = jnp.where(is_bwd, mine[::-1], mine)
    logs, states = split_packed(ordered)
    acc = (jnp.zeros_like(logs[0]), jnp.zeros_like(states[0]))
    pre = []
    for k in range(ROW):
        pre.append(acc)
        acc = combine(acc, (logs[k], states[k]))
    rows = lax.axis_size("z")
    total = acc
    entering = (jnp.zeros_like(acc[0]), jnp.zeros_like(acc[1]))
    d = 1
    while d < rows:
        pairs = []
        for z in range(rows):
            for x in range(parts):
                to = z + d if x < parts // 2 else z - d
                if 0 <= to < rows:
                    pairs.append((z * parts + x, to * parts + x))
        got = split_packed(lax.ppermute(pack(*total), ("z", "x"), pairs))
        entering = combine(got, entering)
        if d * 2 < rows:
            total = combine(got, total)
        d *= 2
    out = jnp.stack([combine(entering, pre[k])[1] for k in range(ROW)])
    out = jnp.where(is_bwd, out[::-1], out).astype(jnp.bfloat16)
    back = lax.all_to_all(out, "x", 0, 0, tiled=True)
    back = back.reshape(2, H, P_SIZE, N)
    return back[0], back[1], weight_row


def gather_weight(weight_row):
    whole = lax.all_gather(weight_row, "z", axis=0)
    return whole.transpose(2, 0, 1, 3).reshape(weight_row.shape[1], -1)


def per_device(
    frame_inputs,
    gate_channels,
    state_input_weight,
    state_output_weight,
    head_decay_codes,
    loss_frames,
    gated_norm_gain,
    output_weight,
    seam_taper_shape,
):
    frames = frame_inputs[0]
    frame_count = frames.shape[0]
    rows = lax.axis_size("z")
    row_len = lax.axis_size("x")
    chain_length = rows * row_len
    window_length = frame_count * chain_length
    seam_length = SEAM_DEVS * frame_count
    group_count = H // 4
    decay_rate_pair = decay_rates(head_decay_codes, window_length)
    loss_float = loss_frames[0].astype(jnp.float32)[:, None]
    forward_log_decay = -(decay_rate_pair[0][None, :] + STATE_LOSS * loss_float)
    backward_log_decay = -(decay_rate_pair[1][None, :] + STATE_LOSS * loss_float)
    running_fwd = jnp.cumsum(forward_log_decay, axis=0)
    running_bwd = jnp.flip(jnp.cumsum(jnp.flip(backward_log_decay, 0), axis=0), 0)
    b_rows = state_input_weight[0]
    c_rows = state_output_weight[0]
    head_frames = frames.reshape(frame_count, H, P_SIZE)
    b_float = b_rows.astype(jnp.float32)[:, None, :]
    weighted_fwd = (jnp.exp(running_fwd[-1][None, :] - running_fwd)[:, :, None] * b_float).astype(
        jnp.bfloat16
    )
    weighted_bwd = (jnp.exp(running_bwd[0][None, :] - running_bwd)[:, :, None] * b_float).astype(
        jnp.bfloat16
    )
    fresh_fwd = jnp.einsum(
        "shp,shn->hpn", head_frames, weighted_fwd, preferred_element_type=jnp.float32
    )
    fresh_bwd = jnp.einsum(
        "shp,shn->hpn", head_frames, weighted_bwd, preferred_element_type=jnp.float32
    )
    state_fwd, state_bwd, weight_row = scan_states(
        running_fwd[-1], running_bwd[0], fresh_fwd, fresh_bwd, output_weight
    )
    scores = jnp.dot(c_rows, b_rows.T, preferred_element_type=jnp.float32)
    lower_mask = jnp.arange(frame_count)[:, None] >= jnp.arange(frame_count)[None, :]

    def group_mix(group_items):
        group_fwd, group_bwd, group_frames = group_items
        exponent = jnp.where(
            lower_mask[None],
            group_fwd[:, :, None] - group_fwd[:, None, :],
            group_bwd[:, :, None] - group_bwd[:, None, :],
        )
        mixing = (scores[None] * jnp.exp(exponent)).astype(jnp.bfloat16)
        return jnp.einsum("hts,shp->thp", mixing, group_frames, preferred_element_type=jnp.float32)

    grouped_fwd = running_fwd.T.reshape(group_count, 4, frame_count)
    grouped_bwd = running_bwd.T.reshape(group_count, 4, frame_count)
    grouped_frames = head_frames.reshape(frame_count, group_count, 4, P_SIZE).transpose(1, 0, 2, 3)
    local_groups = lax.map(group_mix, (grouped_fwd, grouped_bwd, grouped_frames))
    local_part = local_groups.transpose(1, 0, 2, 3).reshape(frame_count, H, P_SIZE)
    carried_fwd = jnp.exp(running_fwd)[:, :, None] * jnp.einsum(
        "hpn,tn->thp", state_fwd, c_rows, preferred_element_type=jnp.float32
    )
    carried_bwd = jnp.exp(running_bwd)[:, :, None] * jnp.einsum(
        "hpn,tn->thp", state_bwd, c_rows, preferred_element_type=jnp.float32
    )
    summed = local_part + carried_fwd + carried_bwd
    gated_rows = summed * jax.nn.silu(gate_channels[0].astype(jnp.float32)).reshape(
        frame_count, H, P_SIZE
    )
    inverse_rms = lax.rsqrt(jnp.mean(gated_rows * gated_rows, axis=-1, keepdims=True) + EPSILON)
    normed = (
        (gated_rows * inverse_rms).reshape(frame_count, H * P_SIZE) * gated_norm_gain[None, :]
    ).astype(jnp.bfloat16)
    projected_rows = jnp.dot(
        normed,
        gather_weight(weight_row),
        preferred_element_type=jnp.float32,
    ).astype(jnp.bfloat16)
    window_index = lax.axis_index("win")
    window_total = lax.axis_size("win")
    row_index = lax.axis_index("z")
    pairs = []
    for w in range(1, window_total):
        pairs.append(((w - 1) * rows + rows - 1, w * rows))
        pairs.append((w * rows, (w - 1) * rows + rows - 1))
    partner = lax.ppermute(projected_rows, ("win", "z"), pairs)
    seam_pos = lax.axis_index("x") * frame_count + jnp.arange(frame_count)
    is_tail = row_index == rows - 1
    fade_window = jnp.minimum(window_index + is_tail.astype(jnp.int32), window_total - 1)
    fade = taper_weight(seam_taper_shape[fade_window], seam_pos, seam_length)[:, None]
    own_rows = projected_rows.astype(jnp.float32)
    other_rows = partner.astype(jnp.float32)
    head_mix = fade * own_rows + (1.0 - fade) * other_rows
    tail_mix = fade * other_rows + (1.0 - fade) * own_rows
    use_head = (row_index == 0) & (window_index > 0)
    use_tail = is_tail & (window_index < window_total - 1)
    mixed = jnp.where(use_head, head_mix, jnp.where(use_tail, tail_mix, own_rows))
    return mixed.astype(jnp.bfloat16)[None]


def solution(mesh):
    wins, chain = mesh.devices.shape
    rows = chain // ROW
    grid = Mesh(mesh.devices.reshape(wins, rows, ROW), ("win", "z", "x"))
    blocks = ("z", "x")
    in_specs = (
        P("win", blocks, None),
        P("win", blocks, None),
        P("win", blocks, None),
        P("win", blocks, None),
        P(),
        P("win", blocks),
        P(),
        P(None, blocks),
        P(),
    )
    out_specs = P("win", blocks, None)
    return jax.shard_map(
        per_device, mesh=grid, in_specs=in_specs, out_specs=out_specs, check_vma=False
    )
```

```python
import jax
import jax.numpy as jnp
from jax import lax
from jax.sharding import Mesh
from jax.sharding import PartitionSpec as P

H = 32
P_SIZE = 64
N = 128
SEAM_DEVS = 4
ROW = 4
PAD_ROWS = 8

STATE_LOSS = 0.4
EPSILON = 1e-05


def decay_rates(head_decay_codes, window_length):
    codes_float = head_decay_codes.astype(jnp.float32)
    quick = jnp.exp2(-codes_float) / 32.0
    gentle = jnp.exp2(5.0 - codes_float) / window_length
    return jnp.where(head_decay_codes < 4, quick, gentle)


def taper_weight(taper_code, position, seam_length):
    spread = (position.astype(jnp.float32) + 0.5) / seam_length
    shapes = jnp.stack(
        [
            spread,
            spread * spread * (3.0 - 2.0 * spread),
            jnp.sin(0.5 * jnp.pi * spread) ** 2,
            spread**3 * (spread * (6.0 * spread - 15.0) + 10.0),
        ]
    )
    kind_index = jnp.arange(4).reshape((4,) + (1,) * spread.ndim)
    selected = kind_index == jnp.expand_dims(taper_code, 0)
    return jnp.sum(jnp.where(selected, shapes, 0.0), axis=0)


def combine(earlier, later):
    return (earlier[0] + later[0], jnp.exp(later[0])[..., None, None] * earlier[1] + later[1])


def shift(value, axis, by):
    count = lax.axis_size(axis)
    pairs = [(i, i + by) for i in range(count) if 0 <= i + by < count]
    return lax.ppermute(value, axis, pairs)


def split_packed(packed):
    return packed[..., P_SIZE, 0], packed[..., :P_SIZE, :]


def pack(logs, states):
    rows = jnp.broadcast_to(logs[..., None, None], logs.shape + (PAD_ROWS, N))
    return jnp.concatenate([states, rows], axis=-2)


def scan_states(log_fwd, log_bwd, fresh_fwd, fresh_bwd):
    packed = pack(jnp.stack([log_fwd, log_bwd]), jnp.stack([fresh_fwd, fresh_bwd]))
    parts = lax.axis_size("x")
    per_part = 2 * H // parts
    packed = packed.reshape(parts, per_part, P_SIZE + PAD_ROWS, N)
    mine = lax.all_to_all(packed, "x", 0, 0, tiled=True)
    is_bwd = lax.axis_index("x") >= parts // 2
    ordered = jnp.where(is_bwd, mine[::-1], mine)
    logs, states = split_packed(ordered)
    acc = (jnp.zeros_like(logs[0]), jnp.zeros_like(states[0]))
    pre = []
    for k in range(ROW):
        pre.append(acc)
        acc = combine(acc, (logs[k], states[k]))
    rows = lax.axis_size("z")
    total = acc
    entering = (jnp.zeros_like(acc[0]), jnp.zeros_like(acc[1]))
    d = 1
    while d < rows:
        pairs = []
        for z in range(rows):
            for x in range(parts):
                to = z + d if x < parts // 2 else z - d
                if 0 <= to < rows:
                    pairs.append((z * parts + x, to * parts + x))
        got = split_packed(lax.ppermute(pack(*total), ("z", "x"), pairs))
        entering = combine(got, entering)
        if d * 2 < rows:
            total = combine(got, total)
        d *= 2
    out = jnp.stack([combine(entering, pre[k])[1] for k in range(ROW)])
    out = jnp.where(is_bwd, out[::-1], out)
    back = lax.all_to_all(out, "x", 0, 0, tiled=True)
    back = back.reshape(2, H, P_SIZE, N)
    return back[0], back[1]


def gather_weight(output_weight):
    half = lax.axis_index("win") % 2
    half_rows = output_weight.shape[0] // 2
    mine = lax.dynamic_slice_in_dim(output_weight, half * half_rows, half_rows, axis=0)
    column = lax.all_gather(mine, "z", axis=0)
    row = lax.all_gather(column, "x", axis=1)
    gathered = row.transpose(2, 0, 1, 3).reshape(half_rows, -1)
    wins = lax.axis_size("win")
    pairs = [(w, w ^ 1) for w in range(wins)]
    other = lax.ppermute(gathered, "win", pairs)
    return jnp.where(
        half == 0,
        jnp.concatenate([gathered, other], axis=0),
        jnp.concatenate([other, gathered], axis=0),
    )


def per_device(
    frame_inputs,
    gate_channels,
    state_input_weight,
    state_output_weight,
    head_decay_codes,
    loss_frames,
    gated_norm_gain,
    output_weight,
    seam_taper_shape,
):
    frames = frame_inputs[0]
    frame_count = frames.shape[0]
    rows = lax.axis_size("z")
    row_len = lax.axis_size("x")
    chain_length = rows * row_len
    window_length = frame_count * chain_length
    seam_length = SEAM_DEVS * frame_count
    group_count = H // 4
    decay_rate_pair = decay_rates(head_decay_codes, window_length)
    loss_float = loss_frames[0].astype(jnp.float32)[:, None]
    forward_log_decay = -(decay_rate_pair[0][None, :] + STATE_LOSS * loss_float)
    backward_log_decay = -(decay_rate_pair[1][None, :] + STATE_LOSS * loss_float)
    running_fwd = jnp.cumsum(forward_log_decay, axis=0)
    running_bwd = jnp.flip(jnp.cumsum(jnp.flip(backward_log_decay, 0), axis=0), 0)
    b_rows = state_input_weight[0]
    c_rows = state_output_weight[0]
    head_frames = frames.reshape(frame_count, H, P_SIZE)
    b_float = b_rows.astype(jnp.float32)[:, None, :]
    weighted_fwd = (jnp.exp(running_fwd[-1][None, :] - running_fwd)[:, :, None] * b_float).astype(
        jnp.bfloat16
    )
    weighted_bwd = (jnp.exp(running_bwd[0][None, :] - running_bwd)[:, :, None] * b_float).astype(
        jnp.bfloat16
    )
    fresh_fwd = jnp.einsum(
        "shp,shn->hpn", head_frames, weighted_fwd, preferred_element_type=jnp.float32
    )
    fresh_bwd = jnp.einsum(
        "shp,shn->hpn", head_frames, weighted_bwd, preferred_element_type=jnp.float32
    )
    state_fwd, state_bwd = scan_states(running_fwd[-1], running_bwd[0], fresh_fwd, fresh_bwd)
    scores = jnp.dot(c_rows, b_rows.T, preferred_element_type=jnp.float32)
    lower_mask = jnp.arange(frame_count)[:, None] >= jnp.arange(frame_count)[None, :]

    def group_mix(group_items):
        group_fwd, group_bwd, group_frames = group_items
        exponent = jnp.where(
            lower_mask[None],
            group_fwd[:, :, None] - group_fwd[:, None, :],
            group_bwd[:, :, None] - group_bwd[:, None, :],
        )
        mixing = (scores[None] * jnp.exp(exponent)).astype(jnp.bfloat16)
        return jnp.einsum("hts,shp->thp", mixing, group_frames, preferred_element_type=jnp.float32)

    grouped_fwd = running_fwd.T.reshape(group_count, 4, frame_count)
    grouped_bwd = running_bwd.T.reshape(group_count, 4, frame_count)
    grouped_frames = head_frames.reshape(frame_count, group_count, 4, P_SIZE).transpose(1, 0, 2, 3)
    local_groups = lax.map(group_mix, (grouped_fwd, grouped_bwd, grouped_frames))
    local_part = local_groups.transpose(1, 0, 2, 3).reshape(frame_count, H, P_SIZE)
    c_float = c_rows.astype(jnp.float32)
    carried_fwd = jnp.exp(running_fwd)[:, :, None] * jnp.einsum(
        "hpn,tn->thp", state_fwd, c_float, precision=lax.Precision.HIGHEST
    )
    carried_bwd = jnp.exp(running_bwd)[:, :, None] * jnp.einsum(
        "hpn,tn->thp", state_bwd, c_float, precision=lax.Precision.HIGHEST
    )
    summed = local_part + carried_fwd + carried_bwd
    gated_rows = summed * jax.nn.silu(gate_channels[0].astype(jnp.float32)).reshape(
        frame_count, H, P_SIZE
    )
    inverse_rms = lax.rsqrt(jnp.mean(gated_rows * gated_rows, axis=-1, keepdims=True) + EPSILON)
    normed = (
        (gated_rows * inverse_rms).reshape(frame_count, H * P_SIZE) * gated_norm_gain[None, :]
    ).astype(jnp.bfloat16)
    projected_rows = jnp.dot(
        normed,
        gather_weight(output_weight),
        preferred_element_type=jnp.float32,
    ).astype(jnp.bfloat16)
    window_index = lax.axis_index("win")
    window_total = lax.axis_size("win")
    row_index = lax.axis_index("z")
    pairs = []
    for w in range(1, window_total):
        pairs.append(((w - 1) * rows + rows - 1, w * rows))
        pairs.append((w * rows, (w - 1) * rows + rows - 1))
    partner = lax.ppermute(projected_rows, ("win", "z"), pairs)
    seam_pos = lax.axis_index("x") * frame_count + jnp.arange(frame_count)
    is_tail = row_index == rows - 1
    fade_window = jnp.minimum(window_index + is_tail.astype(jnp.int32), window_total - 1)
    fade = taper_weight(seam_taper_shape[fade_window], seam_pos, seam_length)[:, None]
    own_rows = projected_rows.astype(jnp.float32)
    other_rows = partner.astype(jnp.float32)
    head_mix = fade * own_rows + (1.0 - fade) * other_rows
    tail_mix = fade * other_rows + (1.0 - fade) * own_rows
    use_head = (row_index == 0) & (window_index > 0)
    use_tail = is_tail & (window_index < window_total - 1)
    mixed = jnp.where(use_head, head_mix, jnp.where(use_tail, tail_mix, own_rows))
    return mixed.astype(jnp.bfloat16)[None]


def solution(mesh):
    wins, chain = mesh.devices.shape
    rows = chain // ROW
    grid = Mesh(mesh.devices.reshape(wins, rows, ROW), ("win", "z", "x"))
    blocks = ("z", "x")
    in_specs = (
        P("win", blocks, None),
        P("win", blocks, None),
        P("win", blocks, None),
        P("win", blocks, None),
        P(),
        P("win", blocks),
        P(),
        P(None, blocks),
        P(),
    )
    out_specs = P("win", blocks, None)
    return jax.shard_map(
        per_device, mesh=grid, in_specs=in_specs, out_specs=out_specs, check_vma=False
    )
```

```python
import jax
import jax.numpy as jnp
from jax import lax
from jax.sharding import Mesh
from jax.sharding import PartitionSpec as P

H = 32
P_SIZE = 64
N = 128
SEAM_DEVS = 4
ROW = 4
PAD_ROWS = 8

STATE_LOSS = 0.4
EPSILON = 1e-05


def decay_rates(head_decay_codes, window_length):
    codes_float = head_decay_codes.astype(jnp.float32)
    quick = jnp.exp2(-codes_float) / 32.0
    gentle = jnp.exp2(5.0 - codes_float) / window_length
    return jnp.where(head_decay_codes < 4, quick, gentle)


def taper_weight(taper_code, position, seam_length):
    spread = (position.astype(jnp.float32) + 0.5) / seam_length
    shapes = jnp.stack(
        [
            spread,
            spread * spread * (3.0 - 2.0 * spread),
            jnp.sin(0.5 * jnp.pi * spread) ** 2,
            spread**3 * (spread * (6.0 * spread - 15.0) + 10.0),
        ]
    )
    kind_index = jnp.arange(4).reshape((4,) + (1,) * spread.ndim)
    selected = kind_index == jnp.expand_dims(taper_code, 0)
    return jnp.sum(jnp.where(selected, shapes, 0.0), axis=0)


def combine(earlier, later):
    return (earlier[0] + later[0], jnp.exp(later[0])[..., None, None] * earlier[1] + later[1])


def shift(value, axis, by):
    count = lax.axis_size(axis)
    pairs = [(i, i + by) for i in range(count) if 0 <= i + by < count]
    return lax.ppermute(value, axis, pairs)


def split_packed(packed):
    return packed[..., P_SIZE, 0], packed[..., :P_SIZE, :]


def pack(logs, states):
    rows = jnp.broadcast_to(logs[..., None, None], logs.shape + (PAD_ROWS, N))
    return jnp.concatenate([states, rows], axis=-2)


def scan_states(log_fwd, log_bwd, fresh_fwd, fresh_bwd):
    packed = pack(jnp.stack([log_fwd, log_bwd]), jnp.stack([fresh_fwd, fresh_bwd]))
    parts = lax.axis_size("x")
    per_part = 2 * H // parts
    packed = packed.reshape(parts, per_part, P_SIZE + PAD_ROWS, N)
    mine = lax.all_to_all(packed, "x", 0, 0, tiled=True)
    is_bwd = lax.axis_index("x") >= parts // 2
    ordered = jnp.where(is_bwd, mine[::-1], mine)
    logs, states = split_packed(ordered)
    acc = (jnp.zeros_like(logs[0]), jnp.zeros_like(states[0]))
    pre = []
    for k in range(ROW):
        pre.append(acc)
        acc = combine(acc, (logs[k], states[k]))
    rows = lax.axis_size("z")
    total = acc
    entering = (jnp.zeros_like(acc[0]), jnp.zeros_like(acc[1]))
    d = 1
    while d < rows:
        pairs = []
        for z in range(rows):
            for x in range(parts):
                to = z + d if x < parts // 2 else z - d
                if 0 <= to < rows:
                    pairs.append((z * parts + x, to * parts + x))
        got = split_packed(lax.ppermute(pack(*total), ("z", "x"), pairs))
        entering = combine(got, entering)
        if d * 2 < rows:
            total = combine(got, total)
        d *= 2
    out = jnp.stack([combine(entering, pre[k])[1] for k in range(ROW)])
    out = jnp.where(is_bwd, out[::-1], out)
    back = lax.all_to_all(out, "x", 0, 0, tiled=True)
    back = back.reshape(2, H, P_SIZE, N)
    return back[0], back[1]


def gather_weight(output_weight):
    half = lax.axis_index("win") % 2
    half_rows = output_weight.shape[0] // 2
    column = lax.all_gather(output_weight, "z", axis=0)
    mine = lax.dynamic_slice_in_dim(column, half * half_rows, half_rows, axis=1)
    row = lax.all_gather(mine, "x", axis=1)
    gathered = row.transpose(2, 0, 1, 3).reshape(half_rows, -1)
    wins = lax.axis_size("win")
    pairs = [(w, w ^ 1) for w in range(wins)]
    other = lax.ppermute(gathered, "win", pairs)
    return jnp.where(
        half == 0,
        jnp.concatenate([gathered, other], axis=0),
        jnp.concatenate([other, gathered], axis=0),
    )


def per_device(
    frame_inputs,
    gate_channels,
    state_input_weight,
    state_output_weight,
    head_decay_codes,
    loss_frames,
    gated_norm_gain,
    output_weight,
    seam_taper_shape,
):
    frames = frame_inputs[0]
    frame_count = frames.shape[0]
    rows = lax.axis_size("z")
    row_len = lax.axis_size("x")
    chain_length = rows * row_len
    window_length = frame_count * chain_length
    seam_length = SEAM_DEVS * frame_count
    group_count = H // 4
    decay_rate_pair = decay_rates(head_decay_codes, window_length)
    loss_float = loss_frames[0].astype(jnp.float32)[:, None]
    forward_log_decay = -(decay_rate_pair[0][None, :] + STATE_LOSS * loss_float)
    backward_log_decay = -(decay_rate_pair[1][None, :] + STATE_LOSS * loss_float)
    running_fwd = jnp.cumsum(forward_log_decay, axis=0)
    running_bwd = jnp.flip(jnp.cumsum(jnp.flip(backward_log_decay, 0), axis=0), 0)
    b_rows = state_input_weight[0]
    c_rows = state_output_weight[0]
    head_frames = frames.reshape(frame_count, H, P_SIZE)
    b_float = b_rows.astype(jnp.float32)[:, None, :]
    weighted_fwd = (jnp.exp(running_fwd[-1][None, :] - running_fwd)[:, :, None] * b_float).astype(
        jnp.bfloat16
    )
    weighted_bwd = (jnp.exp(running_bwd[0][None, :] - running_bwd)[:, :, None] * b_float).astype(
        jnp.bfloat16
    )
    fresh_fwd = jnp.einsum(
        "shp,shn->hpn", head_frames, weighted_fwd, preferred_element_type=jnp.float32
    )
    fresh_bwd = jnp.einsum(
        "shp,shn->hpn", head_frames, weighted_bwd, preferred_element_type=jnp.float32
    )
    state_fwd, state_bwd = scan_states(running_fwd[-1], running_bwd[0], fresh_fwd, fresh_bwd)
    scores = jnp.dot(c_rows, b_rows.T, preferred_element_type=jnp.float32)
    lower_mask = jnp.arange(frame_count)[:, None] >= jnp.arange(frame_count)[None, :]

    def group_mix(group_items):
        group_fwd, group_bwd, group_frames = group_items
        exponent = jnp.where(
            lower_mask[None],
            group_fwd[:, :, None] - group_fwd[:, None, :],
            group_bwd[:, :, None] - group_bwd[:, None, :],
        )
        mixing = (scores[None] * jnp.exp(exponent)).astype(jnp.bfloat16)
        return jnp.einsum("hts,shp->thp", mixing, group_frames, preferred_element_type=jnp.float32)

    grouped_fwd = running_fwd.T.reshape(group_count, 4, frame_count)
    grouped_bwd = running_bwd.T.reshape(group_count, 4, frame_count)
    grouped_frames = head_frames.reshape(frame_count, group_count, 4, P_SIZE).transpose(1, 0, 2, 3)
    local_groups = lax.map(group_mix, (grouped_fwd, grouped_bwd, grouped_frames))
    local_part = local_groups.transpose(1, 0, 2, 3).reshape(frame_count, H, P_SIZE)
    c_float = c_rows.astype(jnp.float32)
    carried_fwd = jnp.exp(running_fwd)[:, :, None] * jnp.einsum(
        "hpn,tn->thp", state_fwd, c_float, precision=lax.Precision.HIGHEST
    )
    carried_bwd = jnp.exp(running_bwd)[:, :, None] * jnp.einsum(
        "hpn,tn->thp", state_bwd, c_float, precision=lax.Precision.HIGHEST
    )
    summed = local_part + carried_fwd + carried_bwd
    gated_rows = summed * jax.nn.silu(gate_channels[0].astype(jnp.float32)).reshape(
        frame_count, H, P_SIZE
    )
    inverse_rms = lax.rsqrt(jnp.mean(gated_rows * gated_rows, axis=-1, keepdims=True) + EPSILON)
    normed = (
        (gated_rows * inverse_rms).reshape(frame_count, H * P_SIZE) * gated_norm_gain[None, :]
    ).astype(jnp.bfloat16)
    projected_rows = jnp.dot(
        normed,
        gather_weight(output_weight),
        preferred_element_type=jnp.float32,
    ).astype(jnp.bfloat16)
    window_index = lax.axis_index("win")
    window_total = lax.axis_size("win")
    row_index = lax.axis_index("z")
    pairs = []
    for w in range(1, window_total):
        pairs.append(((w - 1) * rows + rows - 1, w * rows))
        pairs.append((w * rows, (w - 1) * rows + rows - 1))
    partner = lax.ppermute(projected_rows, ("win", "z"), pairs)
    seam_pos = lax.axis_index("x") * frame_count + jnp.arange(frame_count)
    is_tail = row_index == rows - 1
    fade_window = jnp.minimum(window_index + is_tail.astype(jnp.int32), window_total - 1)
    fade = taper_weight(seam_taper_shape[fade_window], seam_pos, seam_length)[:, None]
    own_rows = projected_rows.astype(jnp.float32)
    other_rows = partner.astype(jnp.float32)
    head_mix = fade * own_rows + (1.0 - fade) * other_rows
    tail_mix = fade * other_rows + (1.0 - fade) * own_rows
    use_head = (row_index == 0) & (window_index > 0)
    use_tail = is_tail & (window_index < window_total - 1)
    mixed = jnp.where(use_head, head_mix, jnp.where(use_tail, tail_mix, own_rows))
    return mixed.astype(jnp.bfloat16)[None]


def solution(mesh):
    wins, chain = mesh.devices.shape
    rows = chain // ROW
    grid = Mesh(mesh.devices.reshape(wins, rows, ROW), ("win", "z", "x"))
    blocks = ("z", "x")
    in_specs = (
        P("win", blocks, None),
        P("win", blocks, None),
        P("win", blocks, None),
        P("win", blocks, None),
        P(),
        P("win", blocks),
        P(),
        P(None, blocks),
        P(),
    )
    out_specs = P("win", blocks, None)
    return jax.shard_map(
        per_device, mesh=grid, in_specs=in_specs, out_specs=out_specs, check_vma=False
    )
```

```python
import jax
import jax.numpy as jnp
from jax import lax
from jax.sharding import Mesh
from jax.sharding import PartitionSpec as P

H = 32
P_SIZE = 64
N = 128
SEAM_DEVS = 4
ROW = 4
PAD_ROWS = 8

STATE_LOSS = 0.4
EPSILON = 1e-05


def decay_rates(head_decay_codes, window_length):
    codes_float = head_decay_codes.astype(jnp.float32)
    quick = jnp.exp2(-codes_float) / 32.0
    gentle = jnp.exp2(5.0 - codes_float) / window_length
    return jnp.where(head_decay_codes < 4, quick, gentle)


def taper_weight(taper_code, position, seam_length):
    spread = (position.astype(jnp.float32) + 0.5) / seam_length
    shapes = jnp.stack(
        [
            spread,
            spread * spread * (3.0 - 2.0 * spread),
            jnp.sin(0.5 * jnp.pi * spread) ** 2,
            spread**3 * (spread * (6.0 * spread - 15.0) + 10.0),
        ]
    )
    kind_index = jnp.arange(4).reshape((4,) + (1,) * spread.ndim)
    selected = kind_index == jnp.expand_dims(taper_code, 0)
    return jnp.sum(jnp.where(selected, shapes, 0.0), axis=0)


def combine(earlier, later):
    return (earlier[0] + later[0], jnp.exp(later[0])[..., None, None] * earlier[1] + later[1])


def shift(value, axis, by):
    count = lax.axis_size(axis)
    pairs = [(i, i + by) for i in range(count) if 0 <= i + by < count]
    return lax.ppermute(value, axis, pairs)


def split_packed(packed):
    return packed[..., P_SIZE, 0], packed[..., :P_SIZE, :]


def pack(logs, states):
    rows = jnp.broadcast_to(logs[..., None, None], logs.shape + (PAD_ROWS, N))
    return jnp.concatenate([states, rows], axis=-2)


def scan_states(log_fwd, log_bwd, fresh_fwd, fresh_bwd, hold):
    packed = pack(jnp.stack([log_fwd, log_bwd]), jnp.stack([fresh_fwd, fresh_bwd]))
    parts = lax.axis_size("x")
    per_part = 2 * H // parts
    packed = packed.reshape(parts, per_part, P_SIZE + PAD_ROWS, N)
    mine = lax.all_to_all(packed, "x", 0, 0, tiled=True)
    mine, hold = lax.optimization_barrier((mine, hold))
    is_bwd = lax.axis_index("x") >= parts // 2
    ordered = jnp.where(is_bwd, mine[::-1], mine)
    logs, states = split_packed(ordered)
    acc = (jnp.zeros_like(logs[0]), jnp.zeros_like(states[0]))
    pre = []
    for k in range(ROW):
        pre.append(acc)
        acc = combine(acc, (logs[k], states[k]))
    rows = lax.axis_size("z")
    total = acc
    entering = (jnp.zeros_like(acc[0]), jnp.zeros_like(acc[1]))
    d = 1
    while d < rows:
        pairs = []
        for z in range(rows):
            for x in range(parts):
                to = z + d if x < parts // 2 else z - d
                if 0 <= to < rows:
                    pairs.append((z * parts + x, to * parts + x))
        got = split_packed(lax.ppermute(pack(*total), ("z", "x"), pairs))
        entering = combine(got, entering)
        if d * 2 < rows:
            total = combine(got, total)
        d *= 2
    out = jnp.stack([combine(entering, pre[k])[1] for k in range(ROW)])
    out = jnp.where(is_bwd, out[::-1], out)
    back = lax.all_to_all(out, "x", 0, 0, tiled=True)
    back = back.reshape(2, H, P_SIZE, N)
    return back[0], back[1], hold


def gather_weight(output_weight):
    half = lax.axis_index("win") % 2
    half_rows = output_weight.shape[0] // 2
    column = lax.all_gather(output_weight, "z", axis=0)
    mine = lax.dynamic_slice_in_dim(column, half * half_rows, half_rows, axis=1)
    row = lax.all_gather(mine, "x", axis=1)
    gathered = row.transpose(2, 0, 1, 3).reshape(half_rows, -1)
    wins = lax.axis_size("win")
    pairs = [(w, w ^ 1) for w in range(wins)]
    other = lax.ppermute(gathered, "win", pairs)
    return jnp.where(
        half == 0,
        jnp.concatenate([gathered, other], axis=0),
        jnp.concatenate([other, gathered], axis=0),
    )


def per_device(
    frame_inputs,
    gate_channels,
    state_input_weight,
    state_output_weight,
    head_decay_codes,
    loss_frames,
    gated_norm_gain,
    output_weight,
    seam_taper_shape,
):
    frames = frame_inputs[0]
    frame_count = frames.shape[0]
    rows = lax.axis_size("z")
    row_len = lax.axis_size("x")
    chain_length = rows * row_len
    window_length = frame_count * chain_length
    seam_length = SEAM_DEVS * frame_count
    group_count = H // 4
    decay_rate_pair = decay_rates(head_decay_codes, window_length)
    loss_float = loss_frames[0].astype(jnp.float32)[:, None]
    forward_log_decay = -(decay_rate_pair[0][None, :] + STATE_LOSS * loss_float)
    backward_log_decay = -(decay_rate_pair[1][None, :] + STATE_LOSS * loss_float)
    running_fwd = jnp.cumsum(forward_log_decay, axis=0)
    running_bwd = jnp.flip(jnp.cumsum(jnp.flip(backward_log_decay, 0), axis=0), 0)
    b_rows = state_input_weight[0]
    c_rows = state_output_weight[0]
    head_frames = frames.reshape(frame_count, H, P_SIZE)
    b_float = b_rows.astype(jnp.float32)[:, None, :]
    weighted_fwd = (jnp.exp(running_fwd[-1][None, :] - running_fwd)[:, :, None] * b_float).astype(
        jnp.bfloat16
    )
    weighted_bwd = (jnp.exp(running_bwd[0][None, :] - running_bwd)[:, :, None] * b_float).astype(
        jnp.bfloat16
    )
    fresh_fwd = jnp.einsum(
        "shp,shn->hpn", head_frames, weighted_fwd, preferred_element_type=jnp.float32
    )
    fresh_bwd = jnp.einsum(
        "shp,shn->hpn", head_frames, weighted_bwd, preferred_element_type=jnp.float32
    )
    scores = jnp.dot(c_rows, b_rows.T, preferred_element_type=jnp.float32)
    lower_mask = jnp.arange(frame_count)[:, None] >= jnp.arange(frame_count)[None, :]

    def group_mix(group_items):
        group_fwd, group_bwd, group_frames = group_items
        exponent = jnp.where(
            lower_mask[None],
            group_fwd[:, :, None] - group_fwd[:, None, :],
            group_bwd[:, :, None] - group_bwd[:, None, :],
        )
        mixing = (scores[None] * jnp.exp(exponent)).astype(jnp.bfloat16)
        return jnp.einsum("hts,shp->thp", mixing, group_frames, preferred_element_type=jnp.float32)

    grouped_fwd = running_fwd.T.reshape(group_count, 4, frame_count)
    grouped_bwd = running_bwd.T.reshape(group_count, 4, frame_count)
    grouped_frames = head_frames.reshape(frame_count, group_count, 4, P_SIZE).transpose(1, 0, 2, 3)
    local_groups = lax.map(group_mix, (grouped_fwd, grouped_bwd, grouped_frames))
    local_part = local_groups.transpose(1, 0, 2, 3).reshape(frame_count, H, P_SIZE)
    state_fwd, state_bwd, local_part = scan_states(
        running_fwd[-1], running_bwd[0], fresh_fwd, fresh_bwd, local_part
    )
    c_float = c_rows.astype(jnp.float32)
    carried_fwd = jnp.exp(running_fwd)[:, :, None] * jnp.einsum(
        "hpn,tn->thp", state_fwd, c_float, precision=lax.Precision.HIGHEST
    )
    carried_bwd = jnp.exp(running_bwd)[:, :, None] * jnp.einsum(
        "hpn,tn->thp", state_bwd, c_float, precision=lax.Precision.HIGHEST
    )
    summed = local_part + carried_fwd + carried_bwd
    gated_rows = summed * jax.nn.silu(gate_channels[0].astype(jnp.float32)).reshape(
        frame_count, H, P_SIZE
    )
    inverse_rms = lax.rsqrt(jnp.mean(gated_rows * gated_rows, axis=-1, keepdims=True) + EPSILON)
    normed = (
        (gated_rows * inverse_rms).reshape(frame_count, H * P_SIZE) * gated_norm_gain[None, :]
    ).astype(jnp.bfloat16)
    projected_rows = jnp.dot(
        normed,
        gather_weight(output_weight),
        preferred_element_type=jnp.float32,
    ).astype(jnp.bfloat16)
    window_index = lax.axis_index("win")
    window_total = lax.axis_size("win")
    row_index = lax.axis_index("z")
    pairs = []
    for w in range(1, window_total):
        pairs.append(((w - 1) * rows + rows - 1, w * rows))
        pairs.append((w * rows, (w - 1) * rows + rows - 1))
    partner = lax.ppermute(projected_rows, ("win", "z"), pairs)
    seam_pos = lax.axis_index("x") * frame_count + jnp.arange(frame_count)
    is_tail = row_index == rows - 1
    fade_window = jnp.minimum(window_index + is_tail.astype(jnp.int32), window_total - 1)
    fade = taper_weight(seam_taper_shape[fade_window], seam_pos, seam_length)[:, None]
    own_rows = projected_rows.astype(jnp.float32)
    other_rows = partner.astype(jnp.float32)
    head_mix = fade * own_rows + (1.0 - fade) * other_rows
    tail_mix = fade * other_rows + (1.0 - fade) * own_rows
    use_head = (row_index == 0) & (window_index > 0)
    use_tail = is_tail & (window_index < window_total - 1)
    mixed = jnp.where(use_head, head_mix, jnp.where(use_tail, tail_mix, own_rows))
    return mixed.astype(jnp.bfloat16)[None]


def solution(mesh):
    wins, chain = mesh.devices.shape
    rows = chain // ROW
    grid = Mesh(mesh.devices.reshape(wins, rows, ROW), ("win", "z", "x"))
    blocks = ("z", "x")
    in_specs = (
        P("win", blocks, None),
        P("win", blocks, None),
        P("win", blocks, None),
        P("win", blocks, None),
        P(),
        P("win", blocks),
        P(),
        P(None, blocks),
        P(),
    )
    out_specs = P("win", blocks, None)
    return jax.shard_map(
        per_device, mesh=grid, in_specs=in_specs, out_specs=out_specs, check_vma=False
    )
```

```python
import jax
import jax.numpy as jnp
from jax import lax
from jax.sharding import Mesh
from jax.sharding import PartitionSpec as P

H = 32
P_SIZE = 64
N = 128
SEAM_DEVS = 4
ROW = 4
PAD_ROWS = 8

STATE_LOSS = 0.4
EPSILON = 1e-05


def decay_rates(head_decay_codes, window_length):
    codes_float = head_decay_codes.astype(jnp.float32)
    quick = jnp.exp2(-codes_float) / 32.0
    gentle = jnp.exp2(5.0 - codes_float) / window_length
    return jnp.where(head_decay_codes < 4, quick, gentle)


def taper_weight(taper_code, position, seam_length):
    spread = (position.astype(jnp.float32) + 0.5) / seam_length
    shapes = jnp.stack(
        [
            spread,
            spread * spread * (3.0 - 2.0 * spread),
            jnp.sin(0.5 * jnp.pi * spread) ** 2,
            spread**3 * (spread * (6.0 * spread - 15.0) + 10.0),
        ]
    )
    kind_index = jnp.arange(4).reshape((4,) + (1,) * spread.ndim)
    selected = kind_index == jnp.expand_dims(taper_code, 0)
    return jnp.sum(jnp.where(selected, shapes, 0.0), axis=0)


def combine(earlier, later):
    return (earlier[0] + later[0], jnp.exp(later[0])[..., None, None] * earlier[1] + later[1])


def shift(value, axis, by):
    count = lax.axis_size(axis)
    pairs = [(i, i + by) for i in range(count) if 0 <= i + by < count]
    return lax.ppermute(value, axis, pairs)


def split_packed(packed):
    return packed[..., P_SIZE, 0], packed[..., :P_SIZE, :]


def pack(logs, states):
    rows = jnp.broadcast_to(logs[..., None, None], logs.shape + (PAD_ROWS, N))
    return jnp.concatenate([states, rows], axis=-2)


def scan_states(log_fwd, log_bwd, fresh_fwd, fresh_bwd, hold):
    packed = pack(jnp.stack([log_fwd, log_bwd]), jnp.stack([fresh_fwd, fresh_bwd]))
    parts = lax.axis_size("x")
    per_part = 2 * H // parts
    packed = packed.reshape(parts, per_part, P_SIZE + PAD_ROWS, N)
    half = parts // 2
    odd = lax.axis_index("win") % 2 == 1
    send = jnp.where(odd, jnp.concatenate([packed[half:], packed[:half]]), packed)
    mine = lax.all_to_all(send, "x", 0, 0, tiled=True)
    mine, hold = lax.optimization_barrier((mine, hold))
    is_bwd = jnp.logical_xor(lax.axis_index("x") >= half, odd)
    ordered = jnp.where(is_bwd, mine[::-1], mine)
    logs, states = split_packed(ordered)
    acc = (jnp.zeros_like(logs[0]), jnp.zeros_like(states[0]))
    pre = []
    for k in range(ROW):
        pre.append(acc)
        acc = combine(acc, (logs[k], states[k]))
    rows = lax.axis_size("z")
    wins = lax.axis_size("win")
    total = acc
    entering = (jnp.zeros_like(acc[0]), jnp.zeros_like(acc[1]))
    d = 1
    while d < rows:
        pairs = []
        for w in range(wins):
            for z in range(rows):
                for x in range(parts):
                    to = z - d if (x >= half) != (w % 2 == 1) else z + d
                    if 0 <= to < rows:
                        pairs.append(((w * rows + z) * parts + x, (w * rows + to) * parts + x))
        got = split_packed(lax.ppermute(pack(*total), ("win", "z", "x"), pairs))
        entering = combine(got, entering)
        if d * 2 < rows:
            total = combine(got, total)
        d *= 2
    out = jnp.stack([combine(entering, pre[k])[1] for k in range(ROW)])
    out = jnp.where(is_bwd, out[::-1], out)
    back = lax.all_to_all(out, "x", 0, 0, tiled=True)
    back = jnp.where(odd, jnp.concatenate([back[half:], back[:half]]), back)
    back = back.reshape(2, H, P_SIZE, N)
    return back[0], back[1], hold


def gather_weight(output_weight):
    half = lax.axis_index("win") % 2
    half_rows = output_weight.shape[0] // 2
    column = lax.all_gather(output_weight, "z", axis=0)
    mine = lax.dynamic_slice_in_dim(column, half * half_rows, half_rows, axis=1)
    row = lax.all_gather(mine, "x", axis=1)
    gathered = row.transpose(2, 0, 1, 3).reshape(half_rows, -1)
    wins = lax.axis_size("win")
    pairs = [(w, w ^ 1) for w in range(wins)]
    other = lax.ppermute(gathered, "win", pairs)
    return jnp.where(
        half == 0,
        jnp.concatenate([gathered, other], axis=0),
        jnp.concatenate([other, gathered], axis=0),
    )


def per_device(
    frame_inputs,
    gate_channels,
    state_input_weight,
    state_output_weight,
    head_decay_codes,
    loss_frames,
    gated_norm_gain,
    output_weight,
    seam_taper_shape,
):
    frames = frame_inputs[0]
    frame_count = frames.shape[0]
    rows = lax.axis_size("z")
    row_len = lax.axis_size("x")
    chain_length = rows * row_len
    window_length = frame_count * chain_length
    seam_length = SEAM_DEVS * frame_count
    group_count = H // 4
    decay_rate_pair = decay_rates(head_decay_codes, window_length)
    loss_float = loss_frames[0].astype(jnp.float32)[:, None]
    forward_log_decay = -(decay_rate_pair[0][None, :] + STATE_LOSS * loss_float)
    backward_log_decay = -(decay_rate_pair[1][None, :] + STATE_LOSS * loss_float)
    running_fwd = jnp.cumsum(forward_log_decay, axis=0)
    running_bwd = jnp.flip(jnp.cumsum(jnp.flip(backward_log_decay, 0), axis=0), 0)
    b_rows = state_input_weight[0]
    c_rows = state_output_weight[0]
    head_frames = frames.reshape(frame_count, H, P_SIZE)
    b_float = b_rows.astype(jnp.float32)[:, None, :]
    weighted_fwd = (jnp.exp(running_fwd[-1][None, :] - running_fwd)[:, :, None] * b_float).astype(
        jnp.bfloat16
    )
    weighted_bwd = (jnp.exp(running_bwd[0][None, :] - running_bwd)[:, :, None] * b_float).astype(
        jnp.bfloat16
    )
    fresh_fwd = jnp.einsum(
        "shp,shn->hpn", head_frames, weighted_fwd, preferred_element_type=jnp.float32
    )
    fresh_bwd = jnp.einsum(
        "shp,shn->hpn", head_frames, weighted_bwd, preferred_element_type=jnp.float32
    )
    scores = jnp.dot(c_rows, b_rows.T, preferred_element_type=jnp.float32)
    lower_mask = jnp.arange(frame_count)[:, None] >= jnp.arange(frame_count)[None, :]

    def group_mix(group_items):
        group_fwd, group_bwd, group_frames = group_items
        exponent = jnp.where(
            lower_mask[None],
            group_fwd[:, :, None] - group_fwd[:, None, :],
            group_bwd[:, :, None] - group_bwd[:, None, :],
        )
        mixing = (scores[None] * jnp.exp(exponent)).astype(jnp.bfloat16)
        return jnp.einsum("hts,shp->thp", mixing, group_frames, preferred_element_type=jnp.float32)

    grouped_fwd = running_fwd.T.reshape(group_count, 4, frame_count)
    grouped_bwd = running_bwd.T.reshape(group_count, 4, frame_count)
    grouped_frames = head_frames.reshape(frame_count, group_count, 4, P_SIZE).transpose(1, 0, 2, 3)
    local_groups = lax.map(group_mix, (grouped_fwd, grouped_bwd, grouped_frames))
    local_part = local_groups.transpose(1, 0, 2, 3).reshape(frame_count, H, P_SIZE)
    state_fwd, state_bwd, local_part = scan_states(
        running_fwd[-1], running_bwd[0], fresh_fwd, fresh_bwd, local_part
    )
    c_float = c_rows.astype(jnp.float32)
    carried_fwd = jnp.exp(running_fwd)[:, :, None] * jnp.einsum(
        "hpn,tn->thp", state_fwd, c_float, precision=lax.Precision.HIGHEST
    )
    carried_bwd = jnp.exp(running_bwd)[:, :, None] * jnp.einsum(
        "hpn,tn->thp", state_bwd, c_float, precision=lax.Precision.HIGHEST
    )
    summed = local_part + carried_fwd + carried_bwd
    gated_rows = summed * jax.nn.silu(gate_channels[0].astype(jnp.float32)).reshape(
        frame_count, H, P_SIZE
    )
    inverse_rms = lax.rsqrt(jnp.mean(gated_rows * gated_rows, axis=-1, keepdims=True) + EPSILON)
    normed = (
        (gated_rows * inverse_rms).reshape(frame_count, H * P_SIZE) * gated_norm_gain[None, :]
    ).astype(jnp.bfloat16)
    projected_rows = jnp.dot(
        normed,
        gather_weight(output_weight),
        preferred_element_type=jnp.float32,
    ).astype(jnp.bfloat16)
    window_index = lax.axis_index("win")
    window_total = lax.axis_size("win")
    row_index = lax.axis_index("z")
    pairs = []
    for w in range(1, window_total):
        pairs.append(((w - 1) * rows + rows - 1, w * rows))
        pairs.append((w * rows, (w - 1) * rows + rows - 1))
    partner = lax.ppermute(projected_rows, ("win", "z"), pairs)
    seam_pos = lax.axis_index("x") * frame_count + jnp.arange(frame_count)
    is_tail = row_index == rows - 1
    fade_window = jnp.minimum(window_index + is_tail.astype(jnp.int32), window_total - 1)
    fade = taper_weight(seam_taper_shape[fade_window], seam_pos, seam_length)[:, None]
    own_rows = projected_rows.astype(jnp.float32)
    other_rows = partner.astype(jnp.float32)
    head_mix = fade * own_rows + (1.0 - fade) * other_rows
    tail_mix = fade * other_rows + (1.0 - fade) * own_rows
    use_head = (row_index == 0) & (window_index > 0)
    use_tail = is_tail & (window_index < window_total - 1)
    mixed = jnp.where(use_head, head_mix, jnp.where(use_tail, tail_mix, own_rows))
    return mixed.astype(jnp.bfloat16)[None]


def solution(mesh):
    wins, chain = mesh.devices.shape
    rows = chain // ROW
    grid = Mesh(mesh.devices.reshape(wins, rows, ROW), ("win", "z", "x"))
    blocks = ("z", "x")
    in_specs = (
        P("win", blocks, None),
        P("win", blocks, None),
        P("win", blocks, None),
        P("win", blocks, None),
        P(),
        P("win", blocks),
        P(),
        P(None, blocks),
        P(),
    )
    out_specs = P("win", blocks, None)
    return jax.shard_map(
        per_device, mesh=grid, in_specs=in_specs, out_specs=out_specs, check_vma=False
    )
```

```python
import jax
import jax.numpy as jnp
from jax import lax
from jax.sharding import Mesh
from jax.sharding import PartitionSpec as P

H = 32
P_SIZE = 64
N = 128
SEAM_DEVS = 4
ROW = 4
PAD_ROWS = 8

STATE_LOSS = 0.4
EPSILON = 1e-05


def decay_rates(head_decay_codes, window_length):
    codes_float = head_decay_codes.astype(jnp.float32)
    quick = jnp.exp2(-codes_float) / 32.0
    gentle = jnp.exp2(5.0 - codes_float) / window_length
    return jnp.where(head_decay_codes < 4, quick, gentle)


def taper_weight(taper_code, position, seam_length):
    spread = (position.astype(jnp.float32) + 0.5) / seam_length
    shapes = jnp.stack(
        [
            spread,
            spread * spread * (3.0 - 2.0 * spread),
            jnp.sin(0.5 * jnp.pi * spread) ** 2,
            spread**3 * (spread * (6.0 * spread - 15.0) + 10.0),
        ]
    )
    kind_index = jnp.arange(4).reshape((4,) + (1,) * spread.ndim)
    selected = kind_index == jnp.expand_dims(taper_code, 0)
    return jnp.sum(jnp.where(selected, shapes, 0.0), axis=0)


def combine(earlier, later):
    return (earlier[0] + later[0], jnp.exp(later[0])[..., None, None] * earlier[1] + later[1])


def shift(value, axis, by):
    count = lax.axis_size(axis)
    pairs = [(i, i + by) for i in range(count) if 0 <= i + by < count]
    return lax.ppermute(value, axis, pairs)


def split_packed(packed):
    lead = packed.shape[:-2]
    state_rows = packed.shape[-2] - PAD_ROWS
    heads = state_rows // P_SIZE
    states = packed[..., :state_rows, :].reshape(lead + (heads, P_SIZE, N))
    return packed[..., state_rows, :heads], states


def pack(logs, states):
    lead = states.shape[:-3]
    heads = logs.shape[-1]
    flat = states.reshape(lead + (heads * P_SIZE, N))
    widths = [(0, 0)] * len(lead) + [(0, PAD_ROWS * N - heads)]
    block = jnp.pad(logs, widths).reshape(lead + (PAD_ROWS, N))
    return jnp.concatenate([flat, block], axis=-2)


def scan_states(log_fwd, log_bwd, fresh_fwd, fresh_bwd, hold):
    parts = lax.axis_size("x")
    per_part = 2 * H // parts
    packed = pack(
        jnp.stack([log_fwd, log_bwd]).reshape(parts, per_part),
        jnp.stack([fresh_fwd, fresh_bwd]).reshape(parts, per_part, P_SIZE, N),
    )
    half = parts // 2
    odd = lax.axis_index("win") % 2 == 1
    send = jnp.where(odd, jnp.concatenate([packed[half:], packed[:half]]), packed)
    mine = lax.all_to_all(send, "x", 0, 0, tiled=True)
    mine, hold = lax.optimization_barrier((mine, hold))
    is_bwd = jnp.logical_xor(lax.axis_index("x") >= half, odd)
    ordered = jnp.where(is_bwd, mine[::-1], mine)
    logs, states = split_packed(ordered)
    acc = (jnp.zeros_like(logs[0]), jnp.zeros_like(states[0]))
    pre = []
    for k in range(ROW):
        pre.append(acc)
        acc = combine(acc, (logs[k], states[k]))
    rows = lax.axis_size("z")
    wins = lax.axis_size("win")
    total = acc
    entering = (jnp.zeros_like(acc[0]), jnp.zeros_like(acc[1]))
    d = 1
    while d < rows:
        pairs = []
        for w in range(wins):
            for z in range(rows):
                for x in range(parts):
                    to = z - d if (x >= half) != (w % 2 == 1) else z + d
                    if 0 <= to < rows:
                        pairs.append(((w * rows + z) * parts + x, (w * rows + to) * parts + x))
        got = split_packed(lax.ppermute(pack(*total), ("win", "z", "x"), pairs))
        entering = combine(got, entering)
        if d * 2 < rows:
            total = combine(got, total)
        d *= 2
    out = jnp.stack([combine(entering, pre[k])[1] for k in range(ROW)])
    out = jnp.where(is_bwd, out[::-1], out)
    back = lax.all_to_all(out, "x", 0, 0, tiled=True)
    back = jnp.where(odd, jnp.concatenate([back[half:], back[:half]]), back)
    back = back.reshape(2, H, P_SIZE, N)
    return back[0], back[1], hold


def gather_weight(output_weight):
    half = lax.axis_index("win") % 2
    half_rows = output_weight.shape[0] // 2
    column = lax.all_gather(output_weight, "z", axis=0)
    mine = lax.dynamic_slice_in_dim(column, half * half_rows, half_rows, axis=1)
    row = lax.all_gather(mine, "x", axis=1)
    gathered = row.transpose(2, 0, 1, 3).reshape(half_rows, -1)
    wins = lax.axis_size("win")
    pairs = [(w, w ^ 1) for w in range(wins)]
    other = lax.ppermute(gathered, "win", pairs)
    return jnp.where(
        half == 0,
        jnp.concatenate([gathered, other], axis=0),
        jnp.concatenate([other, gathered], axis=0),
    )


def per_device(
    frame_inputs,
    gate_channels,
    state_input_weight,
    state_output_weight,
    head_decay_codes,
    loss_frames,
    gated_norm_gain,
    output_weight,
    seam_taper_shape,
):
    frames = frame_inputs[0]
    frame_count = frames.shape[0]
    rows = lax.axis_size("z")
    row_len = lax.axis_size("x")
    chain_length = rows * row_len
    window_length = frame_count * chain_length
    seam_length = SEAM_DEVS * frame_count
    group_count = H // 4
    decay_rate_pair = decay_rates(head_decay_codes, window_length)
    loss_float = loss_frames[0].astype(jnp.float32)[:, None]
    forward_log_decay = -(decay_rate_pair[0][None, :] + STATE_LOSS * loss_float)
    backward_log_decay = -(decay_rate_pair[1][None, :] + STATE_LOSS * loss_float)
    running_fwd = jnp.cumsum(forward_log_decay, axis=0)
    running_bwd = jnp.flip(jnp.cumsum(jnp.flip(backward_log_decay, 0), axis=0), 0)
    b_rows = state_input_weight[0]
    c_rows = state_output_weight[0]
    head_frames = frames.reshape(frame_count, H, P_SIZE)
    b_float = b_rows.astype(jnp.float32)[:, None, :]
    weighted_fwd = (jnp.exp(running_fwd[-1][None, :] - running_fwd)[:, :, None] * b_float).astype(
        jnp.bfloat16
    )
    weighted_bwd = (jnp.exp(running_bwd[0][None, :] - running_bwd)[:, :, None] * b_float).astype(
        jnp.bfloat16
    )
    fresh_fwd = jnp.einsum(
        "shp,shn->hpn", head_frames, weighted_fwd, preferred_element_type=jnp.float32
    )
    fresh_bwd = jnp.einsum(
        "shp,shn->hpn", head_frames, weighted_bwd, preferred_element_type=jnp.float32
    )
    scores = jnp.dot(c_rows, b_rows.T, preferred_element_type=jnp.float32)
    lower_mask = jnp.arange(frame_count)[:, None] >= jnp.arange(frame_count)[None, :]

    def group_mix(group_items):
        group_fwd, group_bwd, group_frames = group_items
        exponent = jnp.where(
            lower_mask[None],
            group_fwd[:, :, None] - group_fwd[:, None, :],
            group_bwd[:, :, None] - group_bwd[:, None, :],
        )
        mixing = (scores[None] * jnp.exp(exponent)).astype(jnp.bfloat16)
        return jnp.einsum("hts,shp->thp", mixing, group_frames, preferred_element_type=jnp.float32)

    grouped_fwd = running_fwd.T.reshape(group_count, 4, frame_count)
    grouped_bwd = running_bwd.T.reshape(group_count, 4, frame_count)
    grouped_frames = head_frames.reshape(frame_count, group_count, 4, P_SIZE).transpose(1, 0, 2, 3)
    local_groups = lax.map(group_mix, (grouped_fwd, grouped_bwd, grouped_frames))
    local_part = local_groups.transpose(1, 0, 2, 3).reshape(frame_count, H, P_SIZE)
    state_fwd, state_bwd, local_part = scan_states(
        running_fwd[-1], running_bwd[0], fresh_fwd, fresh_bwd, local_part
    )
    c_float = c_rows.astype(jnp.float32)
    carried_fwd = jnp.exp(running_fwd)[:, :, None] * jnp.einsum(
        "hpn,tn->thp", state_fwd, c_float, precision=lax.Precision.HIGHEST
    )
    carried_bwd = jnp.exp(running_bwd)[:, :, None] * jnp.einsum(
        "hpn,tn->thp", state_bwd, c_float, precision=lax.Precision.HIGHEST
    )
    summed = local_part + carried_fwd + carried_bwd
    gated_rows = summed * jax.nn.silu(gate_channels[0].astype(jnp.float32)).reshape(
        frame_count, H, P_SIZE
    )
    inverse_rms = lax.rsqrt(jnp.mean(gated_rows * gated_rows, axis=-1, keepdims=True) + EPSILON)
    normed = (
        (gated_rows * inverse_rms).reshape(frame_count, H * P_SIZE) * gated_norm_gain[None, :]
    ).astype(jnp.bfloat16)
    projected_rows = jnp.dot(
        normed,
        gather_weight(output_weight),
        preferred_element_type=jnp.float32,
    ).astype(jnp.bfloat16)
    window_index = lax.axis_index("win")
    window_total = lax.axis_size("win")
    row_index = lax.axis_index("z")
    pairs = []
    for w in range(1, window_total):
        pairs.append(((w - 1) * rows + rows - 1, w * rows))
        pairs.append((w * rows, (w - 1) * rows + rows - 1))
    partner = lax.ppermute(projected_rows, ("win", "z"), pairs)
    seam_pos = lax.axis_index("x") * frame_count + jnp.arange(frame_count)
    is_tail = row_index == rows - 1
    fade_window = jnp.minimum(window_index + is_tail.astype(jnp.int32), window_total - 1)
    fade = taper_weight(seam_taper_shape[fade_window], seam_pos, seam_length)[:, None]
    own_rows = projected_rows.astype(jnp.float32)
    other_rows = partner.astype(jnp.float32)
    head_mix = fade * own_rows + (1.0 - fade) * other_rows
    tail_mix = fade * other_rows + (1.0 - fade) * own_rows
    use_head = (row_index == 0) & (window_index > 0)
    use_tail = is_tail & (window_index < window_total - 1)
    mixed = jnp.where(use_head, head_mix, jnp.where(use_tail, tail_mix, own_rows))
    return mixed.astype(jnp.bfloat16)[None]


def solution(mesh):
    wins, chain = mesh.devices.shape
    rows = chain // ROW
    grid = Mesh(mesh.devices.reshape(wins, rows, ROW), ("win", "z", "x"))
    blocks = ("z", "x")
    in_specs = (
        P("win", blocks, None),
        P("win", blocks, None),
        P("win", blocks, None),
        P("win", blocks, None),
        P(),
        P("win", blocks),
        P(),
        P(None, blocks),
        P(),
    )
    out_specs = P("win", blocks, None)
    return jax.shard_map(
        per_device, mesh=grid, in_specs=in_specs, out_specs=out_specs, check_vma=False
    )
```

```python
import jax
import jax.numpy as jnp
from jax import lax
from jax.sharding import Mesh
from jax.sharding import PartitionSpec as P

H = 32
P_SIZE = 64
N = 128
SEAM_DEVS = 4
ROW = 4
PAD_ROWS = 8

STATE_LOSS = 0.4
EPSILON = 1e-05


def decay_rates(head_decay_codes, window_length):
    codes_float = head_decay_codes.astype(jnp.float32)
    quick = jnp.exp2(-codes_float) / 32.0
    gentle = jnp.exp2(5.0 - codes_float) / window_length
    return jnp.where(head_decay_codes < 4, quick, gentle)


def taper_weight(taper_code, position, seam_length):
    spread = (position.astype(jnp.float32) + 0.5) / seam_length
    shapes = jnp.stack(
        [
            spread,
            spread * spread * (3.0 - 2.0 * spread),
            jnp.sin(0.5 * jnp.pi * spread) ** 2,
            spread**3 * (spread * (6.0 * spread - 15.0) + 10.0),
        ]
    )
    kind_index = jnp.arange(4).reshape((4,) + (1,) * spread.ndim)
    selected = kind_index == jnp.expand_dims(taper_code, 0)
    return jnp.sum(jnp.where(selected, shapes, 0.0), axis=0)


def combine(earlier, later):
    return (earlier[0] + later[0], jnp.exp(later[0])[..., None, None] * earlier[1] + later[1])


def shift(value, axis, by):
    count = lax.axis_size(axis)
    pairs = [(i, i + by) for i in range(count) if 0 <= i + by < count]
    return lax.ppermute(value, axis, pairs)


def split_packed(packed):
    return packed[..., P_SIZE, 0], packed[..., :P_SIZE, :]


def pack(logs, states):
    rows = jnp.broadcast_to(logs[..., None, None], logs.shape + (PAD_ROWS, N))
    return jnp.concatenate([states, rows], axis=-2)


def scan_states(log_fwd, log_bwd, fresh_fwd, fresh_bwd, hold):
    packed = pack(jnp.stack([log_fwd, log_bwd]), jnp.stack([fresh_fwd, fresh_bwd]))
    parts = lax.axis_size("x")
    per_part = 2 * H // parts
    packed = packed.reshape(parts, per_part, P_SIZE + PAD_ROWS, N)
    half = parts // 2
    odd = lax.axis_index("win") % 2 == 1
    send = jnp.where(odd, jnp.concatenate([packed[half:], packed[:half]]), packed)
    mine = lax.all_to_all(send, "x", 0, 0, tiled=True)
    mine, hold = lax.optimization_barrier((mine, hold))
    is_bwd = jnp.logical_xor(lax.axis_index("x") >= half, odd)
    ordered = jnp.where(is_bwd, mine[::-1], mine)
    logs, states = split_packed(ordered)
    acc = (jnp.zeros_like(logs[0]), jnp.zeros_like(states[0]))
    pre = []
    for k in range(ROW):
        pre.append(acc)
        acc = combine(acc, (logs[k], states[k]))
    rows = lax.axis_size("z")
    wins = lax.axis_size("win")
    total = acc
    entering = (jnp.zeros_like(acc[0]), jnp.zeros_like(acc[1]))
    d = 1
    while d < rows:
        pairs = []
        for w in range(wins):
            for z in range(rows):
                for x in range(parts):
                    to = z - d if (x >= half) != (w % 2 == 1) else z + d
                    if 0 <= to < rows:
                        pairs.append(((w * rows + z) * parts + x, (w * rows + to) * parts + x))
        got = split_packed(lax.ppermute(pack(*total), ("win", "z", "x"), pairs))
        entering = combine(got, entering)
        if d * 2 < rows:
            total = combine(got, total)
        d *= 2
    out = jnp.stack([combine(entering, pre[k])[1] for k in range(ROW)])
    out = jnp.where(is_bwd, out[::-1], out)
    back = lax.all_to_all(out, "x", 0, 0, tiled=True)
    back = jnp.where(odd, jnp.concatenate([back[half:], back[:half]]), back)
    back = back.reshape(2, H, P_SIZE, N)
    return back[0], back[1], hold


def gather_weight(output_weight):
    half = lax.axis_index("win") % 2
    half_rows = output_weight.shape[0] // 2
    column = lax.all_gather(output_weight, "z", axis=0)
    mine = lax.dynamic_slice_in_dim(column, half * half_rows, half_rows, axis=1)
    row = lax.all_gather(mine, "x", axis=1)
    wins = lax.axis_size("win")
    pairs = [(w, w ^ 1) for w in range(wins)]
    other = lax.ppermute(row, "win", pairs)
    return row, other, half


def project(normed, gathered):
    row, other, half = gathered
    half_rows = row.shape[2]
    mine_cols = lax.dynamic_slice_in_dim(normed, half * half_rows, half_rows, axis=1)
    other_cols = lax.dynamic_slice_in_dim(normed, (1 - half) * half_rows, half_rows, axis=1)
    out = jnp.einsum("tr,zxrc->tzxc", mine_cols, row, preferred_element_type=jnp.float32)
    out = out + jnp.einsum("tr,zxrc->tzxc", other_cols, other, preferred_element_type=jnp.float32)
    return out.reshape(normed.shape[0], -1)


def per_device(
    frame_inputs,
    gate_channels,
    state_input_weight,
    state_output_weight,
    head_decay_codes,
    loss_frames,
    gated_norm_gain,
    output_weight,
    seam_taper_shape,
):
    frames = frame_inputs[0]
    frame_count = frames.shape[0]
    rows = lax.axis_size("z")
    row_len = lax.axis_size("x")
    chain_length = rows * row_len
    window_length = frame_count * chain_length
    seam_length = SEAM_DEVS * frame_count
    group_count = H // 4
    decay_rate_pair = decay_rates(head_decay_codes, window_length)
    loss_float = loss_frames[0].astype(jnp.float32)[:, None]
    forward_log_decay = -(decay_rate_pair[0][None, :] + STATE_LOSS * loss_float)
    backward_log_decay = -(decay_rate_pair[1][None, :] + STATE_LOSS * loss_float)
    running_fwd = jnp.cumsum(forward_log_decay, axis=0)
    running_bwd = jnp.flip(jnp.cumsum(jnp.flip(backward_log_decay, 0), axis=0), 0)
    b_rows = state_input_weight[0]
    c_rows = state_output_weight[0]
    head_frames = frames.reshape(frame_count, H, P_SIZE)
    b_float = b_rows.astype(jnp.float32)[:, None, :]
    weighted_fwd = (jnp.exp(running_fwd[-1][None, :] - running_fwd)[:, :, None] * b_float).astype(
        jnp.bfloat16
    )
    weighted_bwd = (jnp.exp(running_bwd[0][None, :] - running_bwd)[:, :, None] * b_float).astype(
        jnp.bfloat16
    )
    fresh_fwd = jnp.einsum(
        "shp,shn->hpn", head_frames, weighted_fwd, preferred_element_type=jnp.float32
    )
    fresh_bwd = jnp.einsum(
        "shp,shn->hpn", head_frames, weighted_bwd, preferred_element_type=jnp.float32
    )
    scores = jnp.dot(c_rows, b_rows.T, preferred_element_type=jnp.float32)
    lower_mask = jnp.arange(frame_count)[:, None] >= jnp.arange(frame_count)[None, :]

    def group_mix(group_items):
        group_fwd, group_bwd, group_frames = group_items
        exponent = jnp.where(
            lower_mask[None],
            group_fwd[:, :, None] - group_fwd[:, None, :],
            group_bwd[:, :, None] - group_bwd[:, None, :],
        )
        mixing = (scores[None] * jnp.exp(exponent)).astype(jnp.bfloat16)
        return jnp.einsum("hts,shp->thp", mixing, group_frames, preferred_element_type=jnp.float32)

    grouped_fwd = running_fwd.T.reshape(group_count, 4, frame_count)
    grouped_bwd = running_bwd.T.reshape(group_count, 4, frame_count)
    grouped_frames = head_frames.reshape(frame_count, group_count, 4, P_SIZE).transpose(1, 0, 2, 3)
    local_groups = lax.map(group_mix, (grouped_fwd, grouped_bwd, grouped_frames))
    local_part = local_groups.transpose(1, 0, 2, 3).reshape(frame_count, H, P_SIZE)
    state_fwd, state_bwd, local_part = scan_states(
        running_fwd[-1], running_bwd[0], fresh_fwd, fresh_bwd, local_part
    )
    c_float = c_rows.astype(jnp.float32)
    carried_fwd = jnp.exp(running_fwd)[:, :, None] * jnp.einsum(
        "hpn,tn->thp", state_fwd, c_float, precision=lax.Precision.HIGHEST
    )
    carried_bwd = jnp.exp(running_bwd)[:, :, None] * jnp.einsum(
        "hpn,tn->thp", state_bwd, c_float, precision=lax.Precision.HIGHEST
    )
    summed = local_part + carried_fwd + carried_bwd
    gated_rows = summed * jax.nn.silu(gate_channels[0].astype(jnp.float32)).reshape(
        frame_count, H, P_SIZE
    )
    inverse_rms = lax.rsqrt(jnp.mean(gated_rows * gated_rows, axis=-1, keepdims=True) + EPSILON)
    normed = (
        (gated_rows * inverse_rms).reshape(frame_count, H * P_SIZE) * gated_norm_gain[None, :]
    ).astype(jnp.bfloat16)
    projected_rows = project(normed, gather_weight(output_weight)).astype(jnp.bfloat16)
    window_index = lax.axis_index("win")
    window_total = lax.axis_size("win")
    row_index = lax.axis_index("z")
    pairs = []
    for w in range(1, window_total):
        pairs.append(((w - 1) * rows + rows - 1, w * rows))
        pairs.append((w * rows, (w - 1) * rows + rows - 1))
    partner = lax.ppermute(projected_rows, ("win", "z"), pairs)
    seam_pos = lax.axis_index("x") * frame_count + jnp.arange(frame_count)
    is_tail = row_index == rows - 1
    fade_window = jnp.minimum(window_index + is_tail.astype(jnp.int32), window_total - 1)
    fade = taper_weight(seam_taper_shape[fade_window], seam_pos, seam_length)[:, None]
    own_rows = projected_rows.astype(jnp.float32)
    other_rows = partner.astype(jnp.float32)
    head_mix = fade * own_rows + (1.0 - fade) * other_rows
    tail_mix = fade * other_rows + (1.0 - fade) * own_rows
    use_head = (row_index == 0) & (window_index > 0)
    use_tail = is_tail & (window_index < window_total - 1)
    mixed = jnp.where(use_head, head_mix, jnp.where(use_tail, tail_mix, own_rows))
    return mixed.astype(jnp.bfloat16)[None]


def solution(mesh):
    wins, chain = mesh.devices.shape
    rows = chain // ROW
    grid = Mesh(mesh.devices.reshape(wins, rows, ROW), ("win", "z", "x"))
    blocks = ("z", "x")
    in_specs = (
        P("win", blocks, None),
        P("win", blocks, None),
        P("win", blocks, None),
        P("win", blocks, None),
        P(),
        P("win", blocks),
        P(),
        P(None, blocks),
        P(),
    )
    out_specs = P("win", blocks, None)
    return jax.shard_map(
        per_device, mesh=grid, in_specs=in_specs, out_specs=out_specs, check_vma=False
    )
```

```python
import jax
import jax.numpy as jnp
from jax import lax
from jax.sharding import Mesh
from jax.sharding import PartitionSpec as P

H = 32
P_SIZE = 64
N = 128
SEAM_DEVS = 4
ROW = 4
PAD_ROWS = 8

STATE_LOSS = 0.4
EPSILON = 1e-05


def decay_rates(head_decay_codes, window_length):
    codes_float = head_decay_codes.astype(jnp.float32)
    quick = jnp.exp2(-codes_float) / 32.0
    gentle = jnp.exp2(5.0 - codes_float) / window_length
    return jnp.where(head_decay_codes < 4, quick, gentle)


def taper_weight(taper_code, position, seam_length):
    spread = (position.astype(jnp.float32) + 0.5) / seam_length
    shapes = jnp.stack(
        [
            spread,
            spread * spread * (3.0 - 2.0 * spread),
            jnp.sin(0.5 * jnp.pi * spread) ** 2,
            spread**3 * (spread * (6.0 * spread - 15.0) + 10.0),
        ]
    )
    kind_index = jnp.arange(4).reshape((4,) + (1,) * spread.ndim)
    selected = kind_index == jnp.expand_dims(taper_code, 0)
    return jnp.sum(jnp.where(selected, shapes, 0.0), axis=0)


def combine(earlier, later):
    return (earlier[0] + later[0], jnp.exp(later[0])[..., None, None] * earlier[1] + later[1])


def shift(value, axis, by):
    count = lax.axis_size(axis)
    pairs = [(i, i + by) for i in range(count) if 0 <= i + by < count]
    return lax.ppermute(value, axis, pairs)


def split_packed(packed):
    return packed[..., P_SIZE, 0], packed[..., :P_SIZE, :]


def pack(logs, states):
    rows = jnp.broadcast_to(logs[..., None, None], logs.shape + (PAD_ROWS, N))
    return jnp.concatenate([states, rows], axis=-2)


def scan_states(log_fwd, log_bwd, fresh_fwd, fresh_bwd, hold, anchor):
    packed = pack(jnp.stack([log_fwd, log_bwd]), jnp.stack([fresh_fwd, fresh_bwd]))
    parts = lax.axis_size("x")
    per_part = 2 * H // parts
    packed = packed.reshape(parts, per_part, P_SIZE + PAD_ROWS, N)
    half = parts // 2
    odd = lax.axis_index("win") % 2 == 1
    send = jnp.where(odd, jnp.concatenate([packed[half:], packed[:half]]), packed)
    mine = lax.all_to_all(send, "x", 0, 0, tiled=True)
    mine, hold = lax.optimization_barrier((mine, hold))
    is_bwd = jnp.logical_xor(lax.axis_index("x") >= half, odd)
    ordered = jnp.where(is_bwd, mine[::-1], mine)
    logs, states = split_packed(ordered)
    acc = (jnp.zeros_like(logs[0]), jnp.zeros_like(states[0]))
    pre = []
    for k in range(ROW):
        pre.append(acc)
        acc = combine(acc, (logs[k], states[k]))
    rows = lax.axis_size("z")
    wins = lax.axis_size("win")
    total = acc
    entering = (jnp.zeros_like(acc[0]), jnp.zeros_like(acc[1]))
    d = 1
    while d < rows:
        pairs = []
        for w in range(wins):
            for z in range(rows):
                for x in range(parts):
                    to = z - d if (x >= half) != (w % 2 == 1) else z + d
                    if 0 <= to < rows:
                        pairs.append(((w * rows + z) * parts + x, (w * rows + to) * parts + x))
        moved = lax.ppermute(pack(*total), ("win", "z", "x"), pairs)
        if d * 2 >= rows:
            moved, anchor = lax.optimization_barrier((moved, anchor))
        got = split_packed(moved)
        entering = combine(got, entering)
        if d * 2 < rows:
            total = combine(got, total)
        d *= 2
    out = jnp.stack([combine(entering, pre[k])[1] for k in range(ROW)])
    out = jnp.where(is_bwd, out[::-1], out)
    back = lax.all_to_all(out, "x", 0, 0, tiled=True)
    back = jnp.where(odd, jnp.concatenate([back[half:], back[:half]]), back)
    back = back.reshape(2, H, P_SIZE, N)
    return back[0], back[1], hold, anchor


def gather_weight(column):
    half = lax.axis_index("win") % 2
    half_rows = column.shape[1] // 2
    mine = lax.dynamic_slice_in_dim(column, half * half_rows, half_rows, axis=1)
    row = lax.all_gather(mine, "x", axis=1)
    wins = lax.axis_size("win")
    pairs = [(w, w ^ 1) for w in range(wins)]
    other = lax.ppermute(row, "win", pairs)
    return row, other, half


def project(normed, gathered):
    row, other, half = gathered
    half_rows = row.shape[2]
    mine_cols = lax.dynamic_slice_in_dim(normed, half * half_rows, half_rows, axis=1)
    other_cols = lax.dynamic_slice_in_dim(normed, (1 - half) * half_rows, half_rows, axis=1)
    out = jnp.einsum("tr,zxrc->tzxc", mine_cols, row, preferred_element_type=jnp.float32)
    out = out + jnp.einsum("tr,zxrc->tzxc", other_cols, other, preferred_element_type=jnp.float32)
    return out.reshape(normed.shape[0], -1)


def per_device(
    frame_inputs,
    gate_channels,
    state_input_weight,
    state_output_weight,
    head_decay_codes,
    loss_frames,
    gated_norm_gain,
    output_weight,
    seam_taper_shape,
):
    frames = frame_inputs[0]
    frame_count = frames.shape[0]
    rows = lax.axis_size("z")
    row_len = lax.axis_size("x")
    chain_length = rows * row_len
    window_length = frame_count * chain_length
    seam_length = SEAM_DEVS * frame_count
    group_count = H // 4
    decay_rate_pair = decay_rates(head_decay_codes, window_length)
    loss_float = loss_frames[0].astype(jnp.float32)[:, None]
    forward_log_decay = -(decay_rate_pair[0][None, :] + STATE_LOSS * loss_float)
    backward_log_decay = -(decay_rate_pair[1][None, :] + STATE_LOSS * loss_float)
    running_fwd = jnp.cumsum(forward_log_decay, axis=0)
    running_bwd = jnp.flip(jnp.cumsum(jnp.flip(backward_log_decay, 0), axis=0), 0)
    b_rows = state_input_weight[0]
    c_rows = state_output_weight[0]
    head_frames = frames.reshape(frame_count, H, P_SIZE)
    b_float = b_rows.astype(jnp.float32)[:, None, :]
    weighted_fwd = (jnp.exp(running_fwd[-1][None, :] - running_fwd)[:, :, None] * b_float).astype(
        jnp.bfloat16
    )
    weighted_bwd = (jnp.exp(running_bwd[0][None, :] - running_bwd)[:, :, None] * b_float).astype(
        jnp.bfloat16
    )
    fresh_fwd = jnp.einsum(
        "shp,shn->hpn", head_frames, weighted_fwd, preferred_element_type=jnp.float32
    )
    fresh_bwd = jnp.einsum(
        "shp,shn->hpn", head_frames, weighted_bwd, preferred_element_type=jnp.float32
    )
    scores = jnp.dot(c_rows, b_rows.T, preferred_element_type=jnp.float32)
    lower_mask = jnp.arange(frame_count)[:, None] >= jnp.arange(frame_count)[None, :]

    def group_mix(group_items):
        group_fwd, group_bwd, group_frames = group_items
        exponent = jnp.where(
            lower_mask[None],
            group_fwd[:, :, None] - group_fwd[:, None, :],
            group_bwd[:, :, None] - group_bwd[:, None, :],
        )
        mixing = (scores[None] * jnp.exp(exponent)).astype(jnp.bfloat16)
        return jnp.einsum("hts,shp->thp", mixing, group_frames, preferred_element_type=jnp.float32)

    grouped_fwd = running_fwd.T.reshape(group_count, 4, frame_count)
    grouped_bwd = running_bwd.T.reshape(group_count, 4, frame_count)
    grouped_frames = head_frames.reshape(frame_count, group_count, 4, P_SIZE).transpose(1, 0, 2, 3)
    local_groups = lax.map(group_mix, (grouped_fwd, grouped_bwd, grouped_frames))
    local_part = local_groups.transpose(1, 0, 2, 3).reshape(frame_count, H, P_SIZE)
    column = lax.all_gather(output_weight, "z", axis=0)
    state_fwd, state_bwd, local_part, column = scan_states(
        running_fwd[-1], running_bwd[0], fresh_fwd, fresh_bwd, local_part, column
    )
    c_float = c_rows.astype(jnp.float32)
    carried_fwd = jnp.exp(running_fwd)[:, :, None] * jnp.einsum(
        "hpn,tn->thp", state_fwd, c_float, precision=lax.Precision.HIGHEST
    )
    carried_bwd = jnp.exp(running_bwd)[:, :, None] * jnp.einsum(
        "hpn,tn->thp", state_bwd, c_float, precision=lax.Precision.HIGHEST
    )
    summed = local_part + carried_fwd + carried_bwd
    gated_rows = summed * jax.nn.silu(gate_channels[0].astype(jnp.float32)).reshape(
        frame_count, H, P_SIZE
    )
    inverse_rms = lax.rsqrt(jnp.mean(gated_rows * gated_rows, axis=-1, keepdims=True) + EPSILON)
    normed = (
        (gated_rows * inverse_rms).reshape(frame_count, H * P_SIZE) * gated_norm_gain[None, :]
    ).astype(jnp.bfloat16)
    projected_rows = project(normed, gather_weight(column)).astype(jnp.bfloat16)
    window_index = lax.axis_index("win")
    window_total = lax.axis_size("win")
    row_index = lax.axis_index("z")
    pairs = []
    for w in range(1, window_total):
        pairs.append(((w - 1) * rows + rows - 1, w * rows))
        pairs.append((w * rows, (w - 1) * rows + rows - 1))
    partner = lax.ppermute(projected_rows, ("win", "z"), pairs)
    seam_pos = lax.axis_index("x") * frame_count + jnp.arange(frame_count)
    is_tail = row_index == rows - 1
    fade_window = jnp.minimum(window_index + is_tail.astype(jnp.int32), window_total - 1)
    fade = taper_weight(seam_taper_shape[fade_window], seam_pos, seam_length)[:, None]
    own_rows = projected_rows.astype(jnp.float32)
    other_rows = partner.astype(jnp.float32)
    head_mix = fade * own_rows + (1.0 - fade) * other_rows
    tail_mix = fade * other_rows + (1.0 - fade) * own_rows
    use_head = (row_index == 0) & (window_index > 0)
    use_tail = is_tail & (window_index < window_total - 1)
    mixed = jnp.where(use_head, head_mix, jnp.where(use_tail, tail_mix, own_rows))
    return mixed.astype(jnp.bfloat16)[None]


def solution(mesh):
    wins, chain = mesh.devices.shape
    rows = chain // ROW
    grid = Mesh(mesh.devices.reshape(wins, rows, ROW), ("win", "z", "x"))
    blocks = ("z", "x")
    in_specs = (
        P("win", blocks, None),
        P("win", blocks, None),
        P("win", blocks, None),
        P("win", blocks, None),
        P(),
        P("win", blocks),
        P(),
        P(None, blocks),
        P(),
    )
    out_specs = P("win", blocks, None)
    return jax.shard_map(
        per_device, mesh=grid, in_specs=in_specs, out_specs=out_specs, check_vma=False
    )
```

```python
import jax
import jax.numpy as jnp
from jax import lax
from jax.sharding import Mesh
from jax.sharding import PartitionSpec as P

H = 32
P_SIZE = 64
N = 128
SEAM_DEVS = 4
ROW = 4
PAD_ROWS = 8

STATE_LOSS = 0.4
EPSILON = 1e-05


def decay_rates(head_decay_codes, window_length):
    codes_float = head_decay_codes.astype(jnp.float32)
    quick = jnp.exp2(-codes_float) / 32.0
    gentle = jnp.exp2(5.0 - codes_float) / window_length
    return jnp.where(head_decay_codes < 4, quick, gentle)


def taper_weight(taper_code, position, seam_length):
    spread = (position.astype(jnp.float32) + 0.5) / seam_length
    shapes = jnp.stack(
        [
            spread,
            spread * spread * (3.0 - 2.0 * spread),
            jnp.sin(0.5 * jnp.pi * spread) ** 2,
            spread**3 * (spread * (6.0 * spread - 15.0) + 10.0),
        ]
    )
    kind_index = jnp.arange(4).reshape((4,) + (1,) * spread.ndim)
    selected = kind_index == jnp.expand_dims(taper_code, 0)
    return jnp.sum(jnp.where(selected, shapes, 0.0), axis=0)


def combine(earlier, later):
    return (earlier[0] + later[0], jnp.exp(later[0])[..., None, None] * earlier[1] + later[1])


def shift(value, axis, by):
    count = lax.axis_size(axis)
    pairs = [(i, i + by) for i in range(count) if 0 <= i + by < count]
    return lax.ppermute(value, axis, pairs)


def split_packed(packed):
    return packed[..., P_SIZE, 0], packed[..., :P_SIZE, :]


def pack(logs, states):
    rows = jnp.broadcast_to(logs[..., None, None], logs.shape + (PAD_ROWS, N))
    return jnp.concatenate([states, rows], axis=-2)


def scan_states(log_fwd, log_bwd, fresh_fwd, fresh_bwd, hold):
    packed = pack(jnp.stack([log_fwd, log_bwd]), jnp.stack([fresh_fwd, fresh_bwd]))
    parts = lax.axis_size("x")
    per_part = 2 * H // parts
    packed = packed.reshape(parts, per_part, P_SIZE + PAD_ROWS, N)
    half = parts // 2
    odd = lax.axis_index("win") % 2 == 1
    send = jnp.where(odd, jnp.concatenate([packed[half:], packed[:half]]), packed)
    mine = lax.all_to_all(send, "x", 0, 0, tiled=True)
    mine, hold = lax.optimization_barrier((mine, hold))
    is_bwd = jnp.logical_xor(lax.axis_index("x") >= half, odd)
    ordered = jnp.where(is_bwd, mine[::-1], mine)
    logs, states = split_packed(ordered)
    acc = (jnp.zeros_like(logs[0]), jnp.zeros_like(states[0]))
    pre = []
    for k in range(ROW):
        pre.append(acc)
        acc = combine(acc, (logs[k], states[k]))
    rows = lax.axis_size("zh") * lax.axis_size("zl")
    wins = lax.axis_size("win")
    total = acc
    entering = (jnp.zeros_like(acc[0]), jnp.zeros_like(acc[1]))
    d = 1
    while d < rows:
        pairs = []
        for w in range(wins):
            for z in range(rows):
                for x in range(parts):
                    to = z - d if (x >= half) != (w % 2 == 1) else z + d
                    if 0 <= to < rows:
                        pairs.append(((w * rows + z) * parts + x, (w * rows + to) * parts + x))
        got = split_packed(lax.ppermute(pack(*total), ("win", "zh", "zl", "x"), pairs))
        entering = combine(got, entering)
        if d * 2 < rows:
            total = combine(got, total)
        d *= 2
    out = jnp.stack([combine(entering, pre[k])[1] for k in range(ROW)])
    out = jnp.where(is_bwd, out[::-1], out)
    back = lax.all_to_all(out, "x", 0, 0, tiled=True)
    back = jnp.where(odd, jnp.concatenate([back[half:], back[:half]]), back)
    back = back.reshape(2, H, P_SIZE, N)
    return back[0], back[1], hold


def gather_weight(output_weight):
    half = lax.axis_index("win") % 2
    half_rows = output_weight.shape[0] // 2
    far = lax.all_gather(output_weight, "zh", axis=0)
    column = lax.all_gather(far, "zl", axis=1).reshape((-1,) + output_weight.shape)
    mine = lax.dynamic_slice_in_dim(column, half * half_rows, half_rows, axis=1)
    row = lax.all_gather(mine, "x", axis=1)
    wins = lax.axis_size("win")
    pairs = [(w, w ^ 1) for w in range(wins)]
    other = lax.ppermute(row, "win", pairs)
    return row, other, half


def project(normed, gathered):
    row, other, half = gathered
    half_rows = row.shape[2]
    mine_cols = lax.dynamic_slice_in_dim(normed, half * half_rows, half_rows, axis=1)
    other_cols = lax.dynamic_slice_in_dim(normed, (1 - half) * half_rows, half_rows, axis=1)
    out = jnp.einsum("tr,zxrc->tzxc", mine_cols, row, preferred_element_type=jnp.float32)
    out = out + jnp.einsum("tr,zxrc->tzxc", other_cols, other, preferred_element_type=jnp.float32)
    return out.reshape(normed.shape[0], -1)


def per_device(
    frame_inputs,
    gate_channels,
    state_input_weight,
    state_output_weight,
    head_decay_codes,
    loss_frames,
    gated_norm_gain,
    output_weight,
    seam_taper_shape,
):
    frames = frame_inputs[0]
    frame_count = frames.shape[0]
    rows = lax.axis_size("zh") * lax.axis_size("zl")
    row_len = lax.axis_size("x")
    chain_length = rows * row_len
    window_length = frame_count * chain_length
    seam_length = SEAM_DEVS * frame_count
    group_count = H // 4
    decay_rate_pair = decay_rates(head_decay_codes, window_length)
    loss_float = loss_frames[0].astype(jnp.float32)[:, None]
    forward_log_decay = -(decay_rate_pair[0][None, :] + STATE_LOSS * loss_float)
    backward_log_decay = -(decay_rate_pair[1][None, :] + STATE_LOSS * loss_float)
    running_fwd = jnp.cumsum(forward_log_decay, axis=0)
    running_bwd = jnp.flip(jnp.cumsum(jnp.flip(backward_log_decay, 0), axis=0), 0)
    b_rows = state_input_weight[0]
    c_rows = state_output_weight[0]
    head_frames = frames.reshape(frame_count, H, P_SIZE)
    b_float = b_rows.astype(jnp.float32)[:, None, :]
    weighted_fwd = (jnp.exp(running_fwd[-1][None, :] - running_fwd)[:, :, None] * b_float).astype(
        jnp.bfloat16
    )
    weighted_bwd = (jnp.exp(running_bwd[0][None, :] - running_bwd)[:, :, None] * b_float).astype(
        jnp.bfloat16
    )
    fresh_fwd = jnp.einsum(
        "shp,shn->hpn", head_frames, weighted_fwd, preferred_element_type=jnp.float32
    )
    fresh_bwd = jnp.einsum(
        "shp,shn->hpn", head_frames, weighted_bwd, preferred_element_type=jnp.float32
    )
    scores = jnp.dot(c_rows, b_rows.T, preferred_element_type=jnp.float32)
    lower_mask = jnp.arange(frame_count)[:, None] >= jnp.arange(frame_count)[None, :]

    def group_mix(group_items):
        group_fwd, group_bwd, group_frames = group_items
        exponent = jnp.where(
            lower_mask[None],
            group_fwd[:, :, None] - group_fwd[:, None, :],
            group_bwd[:, :, None] - group_bwd[:, None, :],
        )
        mixing = (scores[None] * jnp.exp(exponent)).astype(jnp.bfloat16)
        return jnp.einsum("hts,shp->thp", mixing, group_frames, preferred_element_type=jnp.float32)

    grouped_fwd = running_fwd.T.reshape(group_count, 4, frame_count)
    grouped_bwd = running_bwd.T.reshape(group_count, 4, frame_count)
    grouped_frames = head_frames.reshape(frame_count, group_count, 4, P_SIZE).transpose(1, 0, 2, 3)
    local_groups = lax.map(group_mix, (grouped_fwd, grouped_bwd, grouped_frames))
    local_part = local_groups.transpose(1, 0, 2, 3).reshape(frame_count, H, P_SIZE)
    state_fwd, state_bwd, local_part = scan_states(
        running_fwd[-1], running_bwd[0], fresh_fwd, fresh_bwd, local_part
    )
    c_float = c_rows.astype(jnp.float32)
    carried_fwd = jnp.exp(running_fwd)[:, :, None] * jnp.einsum(
        "hpn,tn->thp", state_fwd, c_float, precision=lax.Precision.HIGHEST
    )
    carried_bwd = jnp.exp(running_bwd)[:, :, None] * jnp.einsum(
        "hpn,tn->thp", state_bwd, c_float, precision=lax.Precision.HIGHEST
    )
    summed = local_part + carried_fwd + carried_bwd
    gated_rows = summed * jax.nn.silu(gate_channels[0].astype(jnp.float32)).reshape(
        frame_count, H, P_SIZE
    )
    inverse_rms = lax.rsqrt(jnp.mean(gated_rows * gated_rows, axis=-1, keepdims=True) + EPSILON)
    normed = (
        (gated_rows * inverse_rms).reshape(frame_count, H * P_SIZE) * gated_norm_gain[None, :]
    ).astype(jnp.bfloat16)
    projected_rows = project(normed, gather_weight(output_weight)).astype(jnp.bfloat16)
    window_index = lax.axis_index("win")
    window_total = lax.axis_size("win")
    row_index = lax.axis_index("zh") * lax.axis_size("zl") + lax.axis_index("zl")
    pairs = []
    for w in range(1, window_total):
        pairs.append(((w - 1) * rows + rows - 1, w * rows))
        pairs.append((w * rows, (w - 1) * rows + rows - 1))
    partner = lax.ppermute(projected_rows, ("win", "zh", "zl"), pairs)
    seam_pos = lax.axis_index("x") * frame_count + jnp.arange(frame_count)
    is_tail = row_index == rows - 1
    fade_window = jnp.minimum(window_index + is_tail.astype(jnp.int32), window_total - 1)
    fade = taper_weight(seam_taper_shape[fade_window], seam_pos, seam_length)[:, None]
    own_rows = projected_rows.astype(jnp.float32)
    other_rows = partner.astype(jnp.float32)
    head_mix = fade * own_rows + (1.0 - fade) * other_rows
    tail_mix = fade * other_rows + (1.0 - fade) * own_rows
    use_head = (row_index == 0) & (window_index > 0)
    use_tail = is_tail & (window_index < window_total - 1)
    mixed = jnp.where(use_head, head_mix, jnp.where(use_tail, tail_mix, own_rows))
    return mixed.astype(jnp.bfloat16)[None]


def solution(mesh):
    wins, chain = mesh.devices.shape
    rows = chain // ROW
    grid = Mesh(mesh.devices.reshape(wins, 2, rows // 2, ROW), ("win", "zh", "zl", "x"))
    blocks = ("zh", "zl", "x")
    in_specs = (
        P("win", blocks, None),
        P("win", blocks, None),
        P("win", blocks, None),
        P("win", blocks, None),
        P(),
        P("win", blocks),
        P(),
        P(None, blocks),
        P(),
    )
    out_specs = P("win", blocks, None)
    return jax.shard_map(
        per_device, mesh=grid, in_specs=in_specs, out_specs=out_specs, check_vma=False
    )
```

```python
import jax
import jax.numpy as jnp
from jax import lax
from jax.sharding import Mesh
from jax.sharding import PartitionSpec as P

H = 32
P_SIZE = 64
N = 128
SEAM_DEVS = 4
ROW = 4
PAD_ROWS = 8

STATE_LOSS = 0.4
EPSILON = 1e-05


def decay_rates(head_decay_codes, window_length):
    codes_float = head_decay_codes.astype(jnp.float32)
    quick = jnp.exp2(-codes_float) / 32.0
    gentle = jnp.exp2(5.0 - codes_float) / window_length
    return jnp.where(head_decay_codes < 4, quick, gentle)


def taper_weight(taper_code, position, seam_length):
    spread = (position.astype(jnp.float32) + 0.5) / seam_length
    shapes = jnp.stack(
        [
            spread,
            spread * spread * (3.0 - 2.0 * spread),
            jnp.sin(0.5 * jnp.pi * spread) ** 2,
            spread**3 * (spread * (6.0 * spread - 15.0) + 10.0),
        ]
    )
    kind_index = jnp.arange(4).reshape((4,) + (1,) * spread.ndim)
    selected = kind_index == jnp.expand_dims(taper_code, 0)
    return jnp.sum(jnp.where(selected, shapes, 0.0), axis=0)


def combine(earlier, later):
    return (earlier[0] + later[0], jnp.exp(later[0])[..., None, None] * earlier[1] + later[1])


def shift(value, axis, by):
    count = lax.axis_size(axis)
    pairs = [(i, i + by) for i in range(count) if 0 <= i + by < count]
    return lax.ppermute(value, axis, pairs)


def split_packed(packed):
    return packed[..., P_SIZE, 0], packed[..., :P_SIZE, :]


def pack(logs, states):
    rows = jnp.broadcast_to(logs[..., None, None], logs.shape + (PAD_ROWS, N))
    return jnp.concatenate([states, rows], axis=-2)


def scan_states(log_fwd, log_bwd, fresh_fwd, fresh_bwd, hold):
    packed = pack(jnp.stack([log_fwd, log_bwd]), jnp.stack([fresh_fwd, fresh_bwd]))
    parts = lax.axis_size("x")
    per_part = 2 * H // parts
    packed = packed.reshape(parts, per_part, P_SIZE + PAD_ROWS, N)
    half = parts // 2
    odd = lax.axis_index("win") % 2 == 1
    send = jnp.where(odd, jnp.concatenate([packed[half:], packed[:half]]), packed)
    mine = lax.all_to_all(send, "x", 0, 0, tiled=True)
    mine, hold = lax.optimization_barrier((mine, hold))
    is_bwd = jnp.logical_xor(lax.axis_index("x") >= half, odd)
    ordered = jnp.where(is_bwd, mine[::-1], mine)
    logs, states = split_packed(ordered)
    acc = (jnp.zeros_like(logs[0]), jnp.zeros_like(states[0]))
    pre = []
    for k in range(ROW):
        pre.append(acc)
        acc = combine(acc, (logs[k], states[k]))
    rows = lax.axis_size("zh") * lax.axis_size("zl")
    wins = lax.axis_size("win")
    total = acc
    entering = (jnp.zeros_like(acc[0]), jnp.zeros_like(acc[1]))
    d = 1
    while d < rows:
        pairs = []
        for w in range(wins):
            for z in range(rows):
                for x in range(parts):
                    to = z - d if (x >= half) != (w % 2 == 1) else z + d
                    if 0 <= to < rows:
                        pairs.append(((w * rows + z) * parts + x, (w * rows + to) * parts + x))
        got = split_packed(lax.ppermute(pack(*total), ("win", "zh", "zl", "x"), pairs))
        entering = combine(got, entering)
        if d * 2 < rows:
            total = combine(got, total)
        d *= 2
    out = jnp.stack([combine(entering, pre[k])[1] for k in range(ROW)])
    out = jnp.where(is_bwd, out[::-1], out)
    back = lax.all_to_all(out, "x", 0, 0, tiled=True)
    back = jnp.where(odd, jnp.concatenate([back[half:], back[:half]]), back)
    back = back.reshape(2, H, P_SIZE, N)
    return back[0], back[1], hold


def gather_weight(output_weight):
    half = lax.axis_index("win") % 2
    half_rows = output_weight.shape[0] // 2
    width = output_weight.shape[1]
    padded = jnp.concatenate([output_weight, jnp.zeros_like(output_weight)], axis=1)
    near = lax.all_gather(padded, "zl", axis=0)
    both = lax.all_gather(near, "zh", axis=0)
    column = both.reshape((-1,) + padded.shape)[..., :width]
    mine = lax.dynamic_slice_in_dim(column, half * half_rows, half_rows, axis=1)
    row = lax.all_gather(mine, "x", axis=1)
    wins = lax.axis_size("win")
    pairs = [(w, w ^ 1) for w in range(wins)]
    other = lax.ppermute(row, "win", pairs)
    return row, other, half


def project(normed, gathered):
    row, other, half = gathered
    half_rows = row.shape[2]
    mine_cols = lax.dynamic_slice_in_dim(normed, half * half_rows, half_rows, axis=1)
    other_cols = lax.dynamic_slice_in_dim(normed, (1 - half) * half_rows, half_rows, axis=1)
    out = jnp.einsum("tr,zxrc->tzxc", mine_cols, row, preferred_element_type=jnp.float32)
    out = out + jnp.einsum("tr,zxrc->tzxc", other_cols, other, preferred_element_type=jnp.float32)
    return out.reshape(normed.shape[0], -1)


def per_device(
    frame_inputs,
    gate_channels,
    state_input_weight,
    state_output_weight,
    head_decay_codes,
    loss_frames,
    gated_norm_gain,
    output_weight,
    seam_taper_shape,
):
    frames = frame_inputs[0]
    frame_count = frames.shape[0]
    rows = lax.axis_size("zh") * lax.axis_size("zl")
    row_len = lax.axis_size("x")
    chain_length = rows * row_len
    window_length = frame_count * chain_length
    seam_length = SEAM_DEVS * frame_count
    group_count = H // 4
    decay_rate_pair = decay_rates(head_decay_codes, window_length)
    loss_float = loss_frames[0].astype(jnp.float32)[:, None]
    forward_log_decay = -(decay_rate_pair[0][None, :] + STATE_LOSS * loss_float)
    backward_log_decay = -(decay_rate_pair[1][None, :] + STATE_LOSS * loss_float)
    running_fwd = jnp.cumsum(forward_log_decay, axis=0)
    running_bwd = jnp.flip(jnp.cumsum(jnp.flip(backward_log_decay, 0), axis=0), 0)
    b_rows = state_input_weight[0]
    c_rows = state_output_weight[0]
    head_frames = frames.reshape(frame_count, H, P_SIZE)
    b_float = b_rows.astype(jnp.float32)[:, None, :]
    weighted_fwd = (jnp.exp(running_fwd[-1][None, :] - running_fwd)[:, :, None] * b_float).astype(
        jnp.bfloat16
    )
    weighted_bwd = (jnp.exp(running_bwd[0][None, :] - running_bwd)[:, :, None] * b_float).astype(
        jnp.bfloat16
    )
    fresh_fwd = jnp.einsum(
        "shp,shn->hpn", head_frames, weighted_fwd, preferred_element_type=jnp.float32
    )
    fresh_bwd = jnp.einsum(
        "shp,shn->hpn", head_frames, weighted_bwd, preferred_element_type=jnp.float32
    )
    scores = jnp.dot(c_rows, b_rows.T, preferred_element_type=jnp.float32)
    lower_mask = jnp.arange(frame_count)[:, None] >= jnp.arange(frame_count)[None, :]

    def group_mix(group_items):
        group_fwd, group_bwd, group_frames = group_items
        exponent = jnp.where(
            lower_mask[None],
            group_fwd[:, :, None] - group_fwd[:, None, :],
            group_bwd[:, :, None] - group_bwd[:, None, :],
        )
        mixing = (scores[None] * jnp.exp(exponent)).astype(jnp.bfloat16)
        return jnp.einsum("hts,shp->thp", mixing, group_frames, preferred_element_type=jnp.float32)

    grouped_fwd = running_fwd.T.reshape(group_count, 4, frame_count)
    grouped_bwd = running_bwd.T.reshape(group_count, 4, frame_count)
    grouped_frames = head_frames.reshape(frame_count, group_count, 4, P_SIZE).transpose(1, 0, 2, 3)
    local_groups = lax.map(group_mix, (grouped_fwd, grouped_bwd, grouped_frames))
    local_part = local_groups.transpose(1, 0, 2, 3).reshape(frame_count, H, P_SIZE)
    state_fwd, state_bwd, local_part = scan_states(
        running_fwd[-1], running_bwd[0], fresh_fwd, fresh_bwd, local_part
    )
    c_float = c_rows.astype(jnp.float32)
    carried_fwd = jnp.exp(running_fwd)[:, :, None] * jnp.einsum(
        "hpn,tn->thp", state_fwd, c_float, precision=lax.Precision.HIGHEST
    )
    carried_bwd = jnp.exp(running_bwd)[:, :, None] * jnp.einsum(
        "hpn,tn->thp", state_bwd, c_float, precision=lax.Precision.HIGHEST
    )
    summed = local_part + carried_fwd + carried_bwd
    gated_rows = summed * jax.nn.silu(gate_channels[0].astype(jnp.float32)).reshape(
        frame_count, H, P_SIZE
    )
    inverse_rms = lax.rsqrt(jnp.mean(gated_rows * gated_rows, axis=-1, keepdims=True) + EPSILON)
    normed = (
        (gated_rows * inverse_rms).reshape(frame_count, H * P_SIZE) * gated_norm_gain[None, :]
    ).astype(jnp.bfloat16)
    projected_rows = project(normed, gather_weight(output_weight)).astype(jnp.bfloat16)
    window_index = lax.axis_index("win")
    window_total = lax.axis_size("win")
    row_index = lax.axis_index("zh") * lax.axis_size("zl") + lax.axis_index("zl")
    pairs = []
    for w in range(1, window_total):
        pairs.append(((w - 1) * rows + rows - 1, w * rows))
        pairs.append((w * rows, (w - 1) * rows + rows - 1))
    partner = lax.ppermute(projected_rows, ("win", "zh", "zl"), pairs)
    seam_pos = lax.axis_index("x") * frame_count + jnp.arange(frame_count)
    is_tail = row_index == rows - 1
    fade_window = jnp.minimum(window_index + is_tail.astype(jnp.int32), window_total - 1)
    fade = taper_weight(seam_taper_shape[fade_window], seam_pos, seam_length)[:, None]
    own_rows = projected_rows.astype(jnp.float32)
    other_rows = partner.astype(jnp.float32)
    head_mix = fade * own_rows + (1.0 - fade) * other_rows
    tail_mix = fade * other_rows + (1.0 - fade) * own_rows
    use_head = (row_index == 0) & (window_index > 0)
    use_tail = is_tail & (window_index < window_total - 1)
    mixed = jnp.where(use_head, head_mix, jnp.where(use_tail, tail_mix, own_rows))
    return mixed.astype(jnp.bfloat16)[None]


def solution(mesh):
    wins, chain = mesh.devices.shape
    rows = chain // ROW
    grid = Mesh(mesh.devices.reshape(wins, 2, rows // 2, ROW), ("win", "zh", "zl", "x"))
    blocks = ("zh", "zl", "x")
    in_specs = (
        P("win", blocks, None),
        P("win", blocks, None),
        P("win", blocks, None),
        P("win", blocks, None),
        P(),
        P("win", blocks),
        P(),
        P(None, blocks),
        P(),
    )
    out_specs = P("win", blocks, None)
    return jax.shard_map(
        per_device, mesh=grid, in_specs=in_specs, out_specs=out_specs, check_vma=False
    )
```

```python
import jax
import jax.numpy as jnp
from jax import lax
from jax.sharding import Mesh
from jax.sharding import PartitionSpec as P

H = 32
P_SIZE = 64
N = 128
SEAM_DEVS = 4
ROW = 4
PAD_ROWS = 8

STATE_LOSS = 0.4
EPSILON = 1e-05


def decay_rates(head_decay_codes, window_length):
    codes_float = head_decay_codes.astype(jnp.float32)
    quick = jnp.exp2(-codes_float) / 32.0
    gentle = jnp.exp2(5.0 - codes_float) / window_length
    return jnp.where(head_decay_codes < 4, quick, gentle)


def taper_weight(taper_code, position, seam_length):
    spread = (position.astype(jnp.float32) + 0.5) / seam_length
    shapes = jnp.stack(
        [
            spread,
            spread * spread * (3.0 - 2.0 * spread),
            jnp.sin(0.5 * jnp.pi * spread) ** 2,
            spread**3 * (spread * (6.0 * spread - 15.0) + 10.0),
        ]
    )
    kind_index = jnp.arange(4).reshape((4,) + (1,) * spread.ndim)
    selected = kind_index == jnp.expand_dims(taper_code, 0)
    return jnp.sum(jnp.where(selected, shapes, 0.0), axis=0)


def combine(earlier, later):
    return (earlier[0] + later[0], jnp.exp(later[0])[..., None, None] * earlier[1] + later[1])


def shift(value, axis, by):
    count = lax.axis_size(axis)
    pairs = [(i, i + by) for i in range(count) if 0 <= i + by < count]
    return lax.ppermute(value, axis, pairs)


def split_packed(packed):
    return packed[..., P_SIZE, 0], packed[..., :P_SIZE, :]


def pack(logs, states):
    rows = jnp.broadcast_to(logs[..., None, None], logs.shape + (PAD_ROWS, N))
    return jnp.concatenate([states, rows], axis=-2)


def pack_dense(logs, states):
    heads = logs.shape[-1]
    flat = states.reshape(heads * P_SIZE, N)
    block = jnp.pad(logs, (0, PAD_ROWS * N - heads)).reshape(PAD_ROWS, N)
    return jnp.concatenate([flat, block], axis=0)


def split_dense(packed, heads):
    state_rows = heads * P_SIZE
    return packed[state_rows, :heads], packed[:state_rows].reshape(heads, P_SIZE, N)


def scan_states(log_fwd, log_bwd, fresh_fwd, fresh_bwd, hold):
    packed = pack(jnp.stack([log_fwd, log_bwd]), jnp.stack([fresh_fwd, fresh_bwd]))
    parts = lax.axis_size("x")
    per_part = 2 * H // parts
    packed = packed.reshape(parts, per_part, P_SIZE + PAD_ROWS, N)
    half = parts // 2
    odd = lax.axis_index("win") % 2 == 1
    send = jnp.where(odd, jnp.concatenate([packed[half:], packed[:half]]), packed)
    mine = lax.all_to_all(send, "x", 0, 0, tiled=True)
    mine, hold = lax.optimization_barrier((mine, hold))
    is_bwd = jnp.logical_xor(lax.axis_index("x") >= half, odd)
    ordered = jnp.where(is_bwd, mine[::-1], mine)
    logs, states = split_packed(ordered)
    acc = (jnp.zeros_like(logs[0]), jnp.zeros_like(states[0]))
    pre = []
    for k in range(ROW):
        pre.append(acc)
        acc = combine(acc, (logs[k], states[k]))
    rows = lax.axis_size("z")
    wins = lax.axis_size("win")
    total = acc
    entering = (jnp.zeros_like(acc[0]), jnp.zeros_like(acc[1]))
    d = 1
    while d < rows:
        pairs = []
        for w in range(wins):
            for z in range(rows):
                for x in range(parts):
                    to = z - d if (x >= half) != (w % 2 == 1) else z + d
                    if 0 <= to < rows:
                        pairs.append(((w * rows + z) * parts + x, (w * rows + to) * parts + x))
        if d * 2 < rows:
            got = split_packed(lax.ppermute(pack(*total), ("win", "z", "x"), pairs))
        else:
            moved = lax.ppermute(pack_dense(*total), ("win", "z", "x"), pairs)
            got = split_dense(moved, per_part)
        entering = combine(got, entering)
        if d * 2 < rows:
            total = combine(got, total)
        d *= 2
    out = jnp.stack([combine(entering, pre[k])[1] for k in range(ROW)])
    out = jnp.where(is_bwd, out[::-1], out)
    back = lax.all_to_all(out, "x", 0, 0, tiled=True)
    back = jnp.where(odd, jnp.concatenate([back[half:], back[:half]]), back)
    back = back.reshape(2, H, P_SIZE, N)
    return back[0], back[1], hold


def gather_weight(output_weight):
    half = lax.axis_index("win") % 2
    half_rows = output_weight.shape[0] // 2
    column = lax.all_gather(output_weight, "z", axis=0)
    mine = lax.dynamic_slice_in_dim(column, half * half_rows, half_rows, axis=1)
    row = lax.all_gather(mine, "x", axis=1)
    wins = lax.axis_size("win")
    pairs = [(w, w ^ 1) for w in range(wins)]
    other = lax.ppermute(row, "win", pairs)
    return row, other, half


def project(normed, gathered):
    row, other, half = gathered
    half_rows = row.shape[2]
    mine_cols = lax.dynamic_slice_in_dim(normed, half * half_rows, half_rows, axis=1)
    other_cols = lax.dynamic_slice_in_dim(normed, (1 - half) * half_rows, half_rows, axis=1)
    out = jnp.einsum("tr,zxrc->tzxc", mine_cols, row, preferred_element_type=jnp.float32)
    out = out + jnp.einsum("tr,zxrc->tzxc", other_cols, other, preferred_element_type=jnp.float32)
    return out.reshape(normed.shape[0], -1)


def per_device(
    frame_inputs,
    gate_channels,
    state_input_weight,
    state_output_weight,
    head_decay_codes,
    loss_frames,
    gated_norm_gain,
    output_weight,
    seam_taper_shape,
):
    frames = frame_inputs[0]
    frame_count = frames.shape[0]
    rows = lax.axis_size("z")
    row_len = lax.axis_size("x")
    chain_length = rows * row_len
    window_length = frame_count * chain_length
    seam_length = SEAM_DEVS * frame_count
    group_count = H // 4
    decay_rate_pair = decay_rates(head_decay_codes, window_length)
    loss_float = loss_frames[0].astype(jnp.float32)[:, None]
    forward_log_decay = -(decay_rate_pair[0][None, :] + STATE_LOSS * loss_float)
    backward_log_decay = -(decay_rate_pair[1][None, :] + STATE_LOSS * loss_float)
    running_fwd = jnp.cumsum(forward_log_decay, axis=0)
    running_bwd = jnp.flip(jnp.cumsum(jnp.flip(backward_log_decay, 0), axis=0), 0)
    b_rows = state_input_weight[0]
    c_rows = state_output_weight[0]
    head_frames = frames.reshape(frame_count, H, P_SIZE)
    b_float = b_rows.astype(jnp.float32)[:, None, :]
    weighted_fwd = (jnp.exp(running_fwd[-1][None, :] - running_fwd)[:, :, None] * b_float).astype(
        jnp.bfloat16
    )
    weighted_bwd = (jnp.exp(running_bwd[0][None, :] - running_bwd)[:, :, None] * b_float).astype(
        jnp.bfloat16
    )
    fresh_fwd = jnp.einsum(
        "shp,shn->hpn", head_frames, weighted_fwd, preferred_element_type=jnp.float32
    )
    fresh_bwd = jnp.einsum(
        "shp,shn->hpn", head_frames, weighted_bwd, preferred_element_type=jnp.float32
    )
    scores = jnp.dot(c_rows, b_rows.T, preferred_element_type=jnp.float32)
    lower_mask = jnp.arange(frame_count)[:, None] >= jnp.arange(frame_count)[None, :]

    def group_mix(group_items):
        group_fwd, group_bwd, group_frames = group_items
        exponent = jnp.where(
            lower_mask[None],
            group_fwd[:, :, None] - group_fwd[:, None, :],
            group_bwd[:, :, None] - group_bwd[:, None, :],
        )
        mixing = (scores[None] * jnp.exp(exponent)).astype(jnp.bfloat16)
        return jnp.einsum("hts,shp->thp", mixing, group_frames, preferred_element_type=jnp.float32)

    grouped_fwd = running_fwd.T.reshape(group_count, 4, frame_count)
    grouped_bwd = running_bwd.T.reshape(group_count, 4, frame_count)
    grouped_frames = head_frames.reshape(frame_count, group_count, 4, P_SIZE).transpose(1, 0, 2, 3)
    local_groups = lax.map(group_mix, (grouped_fwd, grouped_bwd, grouped_frames))
    local_part = local_groups.transpose(1, 0, 2, 3).reshape(frame_count, H, P_SIZE)
    state_fwd, state_bwd, local_part = scan_states(
        running_fwd[-1], running_bwd[0], fresh_fwd, fresh_bwd, local_part
    )
    c_float = c_rows.astype(jnp.float32)
    carried_fwd = jnp.exp(running_fwd)[:, :, None] * jnp.einsum(
        "hpn,tn->thp", state_fwd, c_float, precision=lax.Precision.HIGHEST
    )
    carried_bwd = jnp.exp(running_bwd)[:, :, None] * jnp.einsum(
        "hpn,tn->thp", state_bwd, c_float, precision=lax.Precision.HIGHEST
    )
    summed = local_part + carried_fwd + carried_bwd
    gated_rows = summed * jax.nn.silu(gate_channels[0].astype(jnp.float32)).reshape(
        frame_count, H, P_SIZE
    )
    inverse_rms = lax.rsqrt(jnp.mean(gated_rows * gated_rows, axis=-1, keepdims=True) + EPSILON)
    normed = (
        (gated_rows * inverse_rms).reshape(frame_count, H * P_SIZE) * gated_norm_gain[None, :]
    ).astype(jnp.bfloat16)
    projected_rows = project(normed, gather_weight(output_weight)).astype(jnp.bfloat16)
    window_index = lax.axis_index("win")
    window_total = lax.axis_size("win")
    row_index = lax.axis_index("z")
    pairs = []
    for w in range(1, window_total):
        pairs.append(((w - 1) * rows + rows - 1, w * rows))
        pairs.append((w * rows, (w - 1) * rows + rows - 1))
    partner = lax.ppermute(projected_rows, ("win", "z"), pairs)
    seam_pos = lax.axis_index("x") * frame_count + jnp.arange(frame_count)
    is_tail = row_index == rows - 1
    fade_window = jnp.minimum(window_index + is_tail.astype(jnp.int32), window_total - 1)
    fade = taper_weight(seam_taper_shape[fade_window], seam_pos, seam_length)[:, None]
    own_rows = projected_rows.astype(jnp.float32)
    other_rows = partner.astype(jnp.float32)
    head_mix = fade * own_rows + (1.0 - fade) * other_rows
    tail_mix = fade * other_rows + (1.0 - fade) * own_rows
    use_head = (row_index == 0) & (window_index > 0)
    use_tail = is_tail & (window_index < window_total - 1)
    mixed = jnp.where(use_head, head_mix, jnp.where(use_tail, tail_mix, own_rows))
    return mixed.astype(jnp.bfloat16)[None]


def solution(mesh):
    wins, chain = mesh.devices.shape
    rows = chain // ROW
    grid = Mesh(mesh.devices.reshape(wins, rows, ROW), ("win", "z", "x"))
    blocks = ("z", "x")
    in_specs = (
        P("win", blocks, None),
        P("win", blocks, None),
        P("win", blocks, None),
        P("win", blocks, None),
        P(),
        P("win", blocks),
        P(),
        P(None, blocks),
        P(),
    )
    out_specs = P("win", blocks, None)
    return jax.shard_map(
        per_device, mesh=grid, in_specs=in_specs, out_specs=out_specs, check_vma=False
    )
```

```python
import jax
import jax.numpy as jnp
from jax import lax
from jax.sharding import Mesh
from jax.sharding import PartitionSpec as P

H = 32
P_SIZE = 64
N = 128
SEAM_DEVS = 4
ROW = 4
PAD_ROWS = 8

STATE_LOSS = 0.4
EPSILON = 1e-05


def decay_rates(head_decay_codes, window_length):
    codes_float = head_decay_codes.astype(jnp.float32)
    quick = jnp.exp2(-codes_float) / 32.0
    gentle = jnp.exp2(5.0 - codes_float) / window_length
    return jnp.where(head_decay_codes < 4, quick, gentle)


def taper_weight(taper_code, position, seam_length):
    spread = (position.astype(jnp.float32) + 0.5) / seam_length
    shapes = jnp.stack(
        [
            spread,
            spread * spread * (3.0 - 2.0 * spread),
            jnp.sin(0.5 * jnp.pi * spread) ** 2,
            spread**3 * (spread * (6.0 * spread - 15.0) + 10.0),
        ]
    )
    kind_index = jnp.arange(4).reshape((4,) + (1,) * spread.ndim)
    selected = kind_index == jnp.expand_dims(taper_code, 0)
    return jnp.sum(jnp.where(selected, shapes, 0.0), axis=0)


def combine(earlier, later):
    return (earlier[0] + later[0], jnp.exp(later[0])[..., None, None] * earlier[1] + later[1])


def shift(value, axis, by):
    count = lax.axis_size(axis)
    pairs = [(i, i + by) for i in range(count) if 0 <= i + by < count]
    return lax.ppermute(value, axis, pairs)


def split_packed(packed):
    return packed[..., P_SIZE, 0], packed[..., :P_SIZE, :]


def pack(logs, states):
    rows = jnp.broadcast_to(logs[..., None, None], logs.shape + (PAD_ROWS, N))
    return jnp.concatenate([states, rows], axis=-2)


def pack_dense(logs, states):
    heads = logs.shape[-1]
    flat = states.reshape(heads * P_SIZE, N)
    block = jnp.pad(logs, (0, PAD_ROWS * N - heads)).reshape(PAD_ROWS, N)
    return jnp.concatenate([flat, block], axis=0)


def split_dense(packed, heads):
    state_rows = heads * P_SIZE
    return packed[state_rows, :heads], packed[:state_rows].reshape(heads, P_SIZE, N)


def scan_states(log_fwd, log_bwd, fresh_fwd, fresh_bwd, hold):
    packed = pack(jnp.stack([log_fwd, log_bwd]), jnp.stack([fresh_fwd, fresh_bwd]))
    parts = lax.axis_size("x")
    per_part = 2 * H // parts
    packed = packed.reshape(parts, per_part, P_SIZE + PAD_ROWS, N)
    half = parts // 2
    odd = lax.axis_index("win") % 2 == 1
    send = jnp.where(odd, jnp.concatenate([packed[half:], packed[:half]]), packed)
    mine = lax.all_to_all(send, "x", 0, 0, tiled=True)
    mine, hold = lax.optimization_barrier((mine, hold))
    is_bwd = jnp.logical_xor(lax.axis_index("x") >= half, odd)
    ordered = jnp.where(is_bwd, mine[::-1], mine)
    logs, states = split_packed(ordered)
    acc = (jnp.zeros_like(logs[0]), jnp.zeros_like(states[0]))
    pre = []
    for k in range(ROW):
        pre.append(acc)
        acc = combine(acc, (logs[k], states[k]))
    rows = lax.axis_size("z")
    wins = lax.axis_size("win")
    total = acc
    entering = (jnp.zeros_like(acc[0]), jnp.zeros_like(acc[1]))
    d = 1
    while d < rows:
        pairs = []
        for w in range(wins):
            for z in range(rows):
                for x in range(parts):
                    to = z - d if (x >= half) != (w % 2 == 1) else z + d
                    if 0 <= to < rows:
                        pairs.append(((w * rows + z) * parts + x, (w * rows + to) * parts + x))
        if d * 2 < rows:
            got = split_packed(lax.ppermute(pack(*total), ("win", "z", "x"), pairs))
        else:
            moved = lax.ppermute(pack_dense(*total), ("win", "z", "x"), pairs)
            got = split_dense(moved, per_part)
        entering = combine(got, entering)
        if d * 2 < rows:
            total = combine(got, total)
        d *= 2
    out = jnp.stack([combine(entering, pre[k])[1] for k in range(ROW)])
    out = jnp.where(is_bwd, out[::-1], out)
    back = lax.all_to_all(out, "x", 0, 0, tiled=True)
    back = jnp.where(odd, jnp.concatenate([back[half:], back[:half]]), back)
    back = back.reshape(2, H, P_SIZE, N)
    return back[0], back[1], hold


def gather_weight(output_weight):
    half = lax.axis_index("win") % 2
    half_rows = output_weight.shape[0] // 2
    column = lax.all_gather(output_weight, "z", axis=0)
    mine = lax.dynamic_slice_in_dim(column, half * half_rows, half_rows, axis=1)
    row = lax.all_gather(mine, "x", axis=2, tiled=True)
    wins = lax.axis_size("win")
    pairs = [(w, w ^ 1) for w in range(wins)]
    other = lax.ppermute(row, "win", pairs)
    return row, other, half


def project(normed, gathered):
    row, other, half = gathered
    half_rows = row.shape[1]
    mine_cols = lax.dynamic_slice_in_dim(normed, half * half_rows, half_rows, axis=1)
    other_cols = lax.dynamic_slice_in_dim(normed, (1 - half) * half_rows, half_rows, axis=1)
    out = jnp.einsum("tr,zrk->tzk", mine_cols, row, preferred_element_type=jnp.float32)
    out = out + jnp.einsum("tr,zrk->tzk", other_cols, other, preferred_element_type=jnp.float32)
    return out.reshape(normed.shape[0], -1)


def per_device(
    frame_inputs,
    gate_channels,
    state_input_weight,
    state_output_weight,
    head_decay_codes,
    loss_frames,
    gated_norm_gain,
    output_weight,
    seam_taper_shape,
):
    frames = frame_inputs[0]
    frame_count = frames.shape[0]
    rows = lax.axis_size("z")
    row_len = lax.axis_size("x")
    chain_length = rows * row_len
    window_length = frame_count * chain_length
    seam_length = SEAM_DEVS * frame_count
    group_count = H // 4
    decay_rate_pair = decay_rates(head_decay_codes, window_length)
    loss_float = loss_frames[0].astype(jnp.float32)[:, None]
    forward_log_decay = -(decay_rate_pair[0][None, :] + STATE_LOSS * loss_float)
    backward_log_decay = -(decay_rate_pair[1][None, :] + STATE_LOSS * loss_float)
    running_fwd = jnp.cumsum(forward_log_decay, axis=0)
    running_bwd = jnp.flip(jnp.cumsum(jnp.flip(backward_log_decay, 0), axis=0), 0)
    b_rows = state_input_weight[0]
    c_rows = state_output_weight[0]
    head_frames = frames.reshape(frame_count, H, P_SIZE)
    b_float = b_rows.astype(jnp.float32)[:, None, :]
    weighted_fwd = (jnp.exp(running_fwd[-1][None, :] - running_fwd)[:, :, None] * b_float).astype(
        jnp.bfloat16
    )
    weighted_bwd = (jnp.exp(running_bwd[0][None, :] - running_bwd)[:, :, None] * b_float).astype(
        jnp.bfloat16
    )
    fresh_fwd = jnp.einsum(
        "shp,shn->hpn", head_frames, weighted_fwd, preferred_element_type=jnp.float32
    )
    fresh_bwd = jnp.einsum(
        "shp,shn->hpn", head_frames, weighted_bwd, preferred_element_type=jnp.float32
    )
    scores = jnp.dot(c_rows, b_rows.T, preferred_element_type=jnp.float32)
    lower_mask = jnp.arange(frame_count)[:, None] >= jnp.arange(frame_count)[None, :]

    def group_mix(group_items):
        group_fwd, group_bwd, group_frames = group_items
        exponent = jnp.where(
            lower_mask[None],
            group_fwd[:, :, None] - group_fwd[:, None, :],
            group_bwd[:, :, None] - group_bwd[:, None, :],
        )
        mixing = (scores[None] * jnp.exp(exponent)).astype(jnp.bfloat16)
        return jnp.einsum("hts,shp->thp", mixing, group_frames, preferred_element_type=jnp.float32)

    grouped_fwd = running_fwd.T.reshape(group_count, 4, frame_count)
    grouped_bwd = running_bwd.T.reshape(group_count, 4, frame_count)
    grouped_frames = head_frames.reshape(frame_count, group_count, 4, P_SIZE).transpose(1, 0, 2, 3)
    local_groups = lax.map(group_mix, (grouped_fwd, grouped_bwd, grouped_frames))
    local_part = local_groups.transpose(1, 0, 2, 3).reshape(frame_count, H, P_SIZE)
    state_fwd, state_bwd, local_part = scan_states(
        running_fwd[-1], running_bwd[0], fresh_fwd, fresh_bwd, local_part
    )
    c_float = c_rows.astype(jnp.float32)
    carried_fwd = jnp.exp(running_fwd)[:, :, None] * jnp.einsum(
        "hpn,tn->thp", state_fwd, c_float, precision=lax.Precision.HIGHEST
    )
    carried_bwd = jnp.exp(running_bwd)[:, :, None] * jnp.einsum(
        "hpn,tn->thp", state_bwd, c_float, precision=lax.Precision.HIGHEST
    )
    summed = local_part + carried_fwd + carried_bwd
    gated_rows = summed * jax.nn.silu(gate_channels[0].astype(jnp.float32)).reshape(
        frame_count, H, P_SIZE
    )
    inverse_rms = lax.rsqrt(jnp.mean(gated_rows * gated_rows, axis=-1, keepdims=True) + EPSILON)
    normed = (
        (gated_rows * inverse_rms).reshape(frame_count, H * P_SIZE) * gated_norm_gain[None, :]
    ).astype(jnp.bfloat16)
    projected_rows = project(normed, gather_weight(output_weight)).astype(jnp.bfloat16)
    window_index = lax.axis_index("win")
    window_total = lax.axis_size("win")
    row_index = lax.axis_index("z")
    pairs = []
    for w in range(1, window_total):
        pairs.append(((w - 1) * rows + rows - 1, w * rows))
        pairs.append((w * rows, (w - 1) * rows + rows - 1))
    partner = lax.ppermute(projected_rows, ("win", "z"), pairs)
    seam_pos = lax.axis_index("x") * frame_count + jnp.arange(frame_count)
    is_tail = row_index == rows - 1
    fade_window = jnp.minimum(window_index + is_tail.astype(jnp.int32), window_total - 1)
    fade = taper_weight(seam_taper_shape[fade_window], seam_pos, seam_length)[:, None]
    own_rows = projected_rows.astype(jnp.float32)
    other_rows = partner.astype(jnp.float32)
    head_mix = fade * own_rows + (1.0 - fade) * other_rows
    tail_mix = fade * other_rows + (1.0 - fade) * own_rows
    use_head = (row_index == 0) & (window_index > 0)
    use_tail = is_tail & (window_index < window_total - 1)
    mixed = jnp.where(use_head, head_mix, jnp.where(use_tail, tail_mix, own_rows))
    return mixed.astype(jnp.bfloat16)[None]


def solution(mesh):
    wins, chain = mesh.devices.shape
    rows = chain // ROW
    grid = Mesh(mesh.devices.reshape(wins, rows, ROW), ("win", "z", "x"))
    blocks = ("z", "x")
    in_specs = (
        P("win", blocks, None),
        P("win", blocks, None),
        P("win", blocks, None),
        P("win", blocks, None),
        P(),
        P("win", blocks),
        P(),
        P(None, blocks),
        P(),
    )
    out_specs = P("win", blocks, None)
    return jax.shard_map(
        per_device, mesh=grid, in_specs=in_specs, out_specs=out_specs, check_vma=False
    )
```
